32 devices in a mesh: tm: 16 (over z, y, x), rows: 2 (over core).
Axes of the slice: x: 2, y: 2, z: 4, core: 2. Of those that a mesh axis runs over, the one named last changes fastest.
Arguments:
- frames: bfloat16 [64, 16, 128, 128], P('tm', 'rows'), may hold values from -6 to 6
- conv_in: bfloat16 [3, 3, 128, 128], replicated, may hold values from -0.09375 to 0.09375
- decay: float32 [64, 128], P('tm'), may hold values from 0.35 to 1, as said below
- conv_out: bfloat16 [3, 3, 128, 128], replicated, may hold values from -0.0234375 to 0.0234375
- skip: float32 [128], replicated, may hold values from -4 to 4
Outputs:
- mixed: bfloat16 [64, 16, 128, 128], P('tm', 'rows')
The draws below stay inside these ranges and needn't reach their ends.
Inputs may be any that keep to these rules, and one draw needn't show every extreme that they name: `decay`: every entry lies strictly between 0 and 1.
All inputs are finite; a program needn't handle non-finite values.
Results may differ from the reference program's by a relative error of at most 0.0045.
Values may be sent and summed in bfloat16 or wider, within the bound.
No kernel may reach another device: no remote copies, remote signals or barrier semaphores. Data moves between devices by JAX's collectives and lax.ppermute only.
A program may use at most 192 MiB of HBM per device.

```python
import math
import jax
import jax.numpy as jnp
from jax import lax

CHANNELS = 128
STATE = 128
WIDTH = 128
HEIGHT = 16
TIME = 64


def draw_decay(key, part):
    k_rate, k_fast, k_jit, k_pos, k_fac = jax.random.split(jax.random.fold_in(key, 7), 5)
    share = 0.5
    fast = jax.random.uniform(k_fast, (STATE,), jnp.float32) < share
    slow_rate = jnp.exp(jax.random.uniform(k_rate, (STATE,), jnp.float32, math.log(0.0005), math.log(0.002)))
    fast_rate = jax.random.uniform(jax.random.fold_in(k_rate, 1), (STATE,), jnp.float32, 0.02, 0.035)
    base = jnp.where(fast, fast_rate, slow_rate)
    jitter = jax.random.uniform(k_jit, (TIME, STATE), jnp.float32, 0.7, 1.4)
    rate = 1.0 - base[None, :] * jitter
    spots = jax.random.permutation(k_pos, TIME)[:4]
    factor = jax.random.uniform(k_fac, (4, STATE), jnp.float32, 0.5, 0.8)
    frame_index = jnp.arange(TIME)[:, None]
    scaled = jnp.ones((TIME, STATE), jnp.float32)
    for which in range(4):
        scaled = scaled * jnp.where(frame_index == spots[which], factor[which][None, :], 1.0)
    return (rate * scaled).astype(jnp.float32)


def shard_levels(own_key, extent, pieces, low, high):
    def one(dim, shards_of):
        draws = jax.random.uniform(jax.random.fold_in(jax.random.fold_in(own_key, 6), dim), (shards_of,), jnp.float32, low / len(pieces), high / len(pieces))
        return jnp.repeat(jnp.exp(draws), extent[dim] // shards_of).reshape((-1,) + (1,) * (len(extent) - dim - 1))

    factor_of = one(*pieces[0])
    for cut in pieces[1:]:
        factor_of = factor_of * one(*cut)
    return factor_of


def noise(rng, dims, deviation, most, shards=(), held_as=jnp.bfloat16):
    factor_of = shard_levels(rng, dims, shards, -0.22, 0.18) if shards else 1.0
    drawn = jax.random.normal(rng, dims, jnp.float32) * deviation * factor_of
    return jnp.minimum(jnp.maximum(drawn, -most), most).astype(held_as)


def setup_inputs(seed: int = 0) -> dict:
    seeds = jax.random.split(jax.random.key(seed), 6)
    frames = noise(seeds[0], (TIME, HEIGHT, WIDTH, CHANNELS), 1.0, 6.0, ((0, 16), (1, 2)))
    conv_in = noise(seeds[1], (3, 3, CHANNELS, STATE), (36 * CHANNELS) ** -0.5, 0.09375)
    decay = draw_decay(jax.random.fold_in(seeds[5], 71), 0)
    conv_out = noise(seeds[3], (3, 3, STATE, CHANNELS), (576 * STATE) ** -0.5, 0.0234375)
    skip = noise(seeds[4], (CHANNELS,), 1.0, 4.0, (), jnp.float32)
    return {"frames": frames, "conv_in": conv_in, "decay": decay, "conv_out": conv_out, "skip": skip}


def conv_bands(padded, weight, rows):
    width = padded.shape[1]
    channels = padded.shape[2]
    columns = jnp.pad(padded, ((0, 0), (1, 1), (0, 0)))
    total = jnp.zeros((rows * width, weight.shape[3]), jnp.float32)
    for down in range(3):
        for across in range(3):
            window = columns[down:down + rows, across:across + width, :].reshape(rows * width, channels)
            total = total + jnp.dot(window, weight[down, across], preferred_element_type=jnp.float32)
    return total.reshape(rows, width, weight.shape[3])


def reference(frames, conv_in, decay, conv_out, skip):
    def advance(state, inputs):
        frame, rate = inputs
        padded = jnp.pad(frame, ((1, 1), (0, 0), (0, 0)))
        drive = conv_bands(padded, conv_in, HEIGHT)
        state = rate * state + drive
        rounded = state.astype(jnp.bfloat16)
        outer = jnp.pad(rounded, ((1, 1), (0, 0), (0, 0)))
        result = conv_bands(outer, conv_out, HEIGHT) + skip * frame.astype(jnp.float32)
        return state, result.astype(jnp.bfloat16)

    start = jnp.zeros((HEIGHT, WIDTH, STATE), jnp.float32)
    _, mixed = lax.scan(advance, start, (frames, decay))
    return mixed
```

```python
import jax
import jax.numpy as jnp
from jax import lax
from jax.sharding import PartitionSpec as P


def extended(x, sides, width):
    for axis, dim in sides:
        size, length = (lax.axis_size(axis), x.shape[dim])
        up = [(i, (i + 1) % size) for i in range(size - 1)]
        down = [(j, i) for i, j in up]
        last = lax.slice_in_dim(x, length - width, length, axis=dim)
        first = lax.slice_in_dim(x, 0, width, axis=dim)
        before = lax.ppermute(last, axis, up)
        after = lax.ppermute(first, axis, down)
        x = jnp.concatenate([before, x, after], axis=dim)
    return x


def conv_rows(padded, weight):
    return lax.conv_general_dilated(
        padded,
        weight,
        window_strides=(1, 1),
        padding=((0, 0), (1, 1)),
        dimension_numbers=("NHWC", "HWIO", "NHWC"),
        preferred_element_type=jnp.float32,
    )


def split3(p):
    hi = lax.reduce_precision(p, exponent_bits=8, mantissa_bits=7)
    rest = p - hi
    mid = lax.reduce_precision(rest, exponent_bits=8, mantissa_bits=7)
    low = rest - mid
    return jnp.stack([hi, mid, low]).astype(jnp.bfloat16)


def incoming_state(power, state, axis):
    n = lax.axis_size(axis)
    rows, width, channels = state.shape
    win_p, win_s = power, state
    acc_p, acc_s = None, None
    shift = 1
    while shift < n:
        pairs = [(i, i + shift) for i in range(n - shift)]
        payload = jnp.concatenate(
            [win_s.astype(jnp.bfloat16).reshape(rows * width, channels), split3(win_p)], axis=0
        )
        got = lax.ppermute(payload, axis, pairs)
        got_s = got[: rows * width].astype(jnp.float32).reshape(rows, width, channels)
        got_p = jnp.sum(got[rows * width :].astype(jnp.float32), axis=0)
        if acc_s is None:
            acc_p, acc_s = got_p, got_s
        else:
            acc_s = acc_p * got_s + acc_s
            acc_p = got_p * acc_p
        if 2 * shift < n:
            win_s = win_p * got_s + win_s
            win_p = got_p * win_p
        shift *= 2
    if acc_s is None:
        return jnp.zeros_like(state)
    return acc_s


def shards(frames, conv_in, decay, conv_out, skip):
    count = frames.shape[0]
    with jax.named_scope("input_conv"):
        padded_in = extended(frames, (("rows", 1),), 1)
        drive = conv_rows(padded_in, conv_in)
    with jax.named_scope("local_recurrence"):
        state = jnp.zeros(drive.shape[1:], jnp.float32)
        power = jnp.ones(decay.shape[1:], jnp.float32)
        local_states = []
        products = []
        for frame_index in range(count):
            state = decay[frame_index] * state + drive[frame_index]
            power = power * decay[frame_index]
            local_states.append(state)
            products.append(power)
        stacked = jnp.stack(local_states)
        cumulative = jnp.stack(products)[:, None, None, :]
    with jax.named_scope("carry_across_blocks"):
        incoming = incoming_state(power, state, "tm")
    with jax.named_scope("output_conv"):
        inner = (stacked + cumulative * incoming[None]).astype(jnp.bfloat16)
        rounded = extended(inner, (("rows", 1),), 1)
        value = conv_rows(rounded, conv_out) + skip * frames.astype(jnp.float32)
    return value.astype(jnp.bfloat16)


def solution(mesh):
    return jax.shard_map(
        shards,
        mesh=mesh,
        in_specs=(P("tm", "rows", None, None), P(), P("tm", None), P(), P()),
        out_specs=P("tm", "rows", None, None),
        check_vma=False,
    )
```

```python
import jax
import jax.numpy as jnp
from jax import lax
from jax.experimental import pallas as pl
from jax.experimental.pallas import tpu as pltpu
from jax.sharding import PartitionSpec as P


def halo_rows(x, axis, dim):
    size, length = (lax.axis_size(axis), x.shape[dim])
    up = [(i, (i + 1) % size) for i in range(size - 1)]
    down = [(j, i) for i, j in up]
    last = lax.slice_in_dim(x, length - 1, length, axis=dim)
    first = lax.slice_in_dim(x, 0, 1, axis=dim)
    before = lax.ppermute(last, axis, up)
    after = lax.ppermute(first, axis, down)
    return before, after


def grouped_taps(weight):
    down, across, k, m = weight.shape
    return jnp.transpose(weight, (0, 2, 1, 3)).reshape(down, k, across * m)


def conv_taps(x, w_ref):
    rows = x.shape[0] - 2
    width, k = x.shape[1], x.shape[2]
    m = w_ref.shape[2] // 3
    n = rows * width
    acc = None
    for a in range(3):
        lhs = x[a : a + rows].reshape(n, k)
        part = jnp.dot(lhs, w_ref[a], preferred_element_type=jnp.float32)
        acc = part if acc is None else acc + part
    column = lax.broadcasted_iota(jnp.int32, (n, m), 0) % width
    from_left = pltpu.roll(acc[:, :m], 1, 0)
    from_right = pltpu.roll(acc[:, 2 * m :], n - 1, 0)
    total = acc[:, m : 2 * m]
    total = total + jnp.where(column == 0, 0.0, from_left)
    total = total + jnp.where(column == width - 1, 0.0, from_right)
    return total


def input_kernel(decay_ref, top_ref, frame_ref, bottom_ref, w_ref, out_ref, state_ref):
    f = pl.program_id(0)
    band, width, m = out_ref.shape[1:]

    @pl.when(f == 0)
    def _():
        state_ref[...] = jnp.zeros_like(state_ref)

    x = jnp.concatenate([top_ref[0], frame_ref[0], bottom_ref[0]], axis=0)
    drive = conv_taps(x, w_ref)
    state = decay_ref[pl.ds(f, 1), :] * state_ref[...] + drive
    state_ref[...] = state
    out_ref[0] = state.reshape(band, width, m)


def output_kernel(
    cum_ref, skip_ref, incoming_ref, top_ref, local_ref, bottom_ref, frame_ref, w_ref, out_ref
):
    f = pl.program_id(0)
    band, width, m = out_ref.shape[1:]
    inner = (local_ref[0] + cum_ref[pl.ds(f, 1), :] * incoming_ref[...]).astype(jnp.bfloat16)
    x = jnp.concatenate([top_ref[0], inner, bottom_ref[0]], axis=0)
    total = conv_taps(x, w_ref)
    frame = frame_ref[0].reshape(band * width, m).astype(jnp.float32)
    total = total + skip_ref[...] * frame
    out_ref[0] = total.astype(jnp.bfloat16).reshape(band, width, m)


def input_stage(frames, conv_in, decay):
    count, band, width, channels = frames.shape
    state_width = conv_in.shape[3]
    top, bottom = halo_rows(frames, "rows", 1)
    halo = pl.BlockSpec((1, 1, width, channels), lambda f: (f, 0, 0, 0))
    return pl.pallas_call(
        input_kernel,
        grid=(count,),
        in_specs=[
            pl.BlockSpec((count, state_width), lambda f: (0, 0)),
            halo,
            pl.BlockSpec((1, band, width, channels), lambda f: (f, 0, 0, 0)),
            halo,
            pl.BlockSpec((3, channels, 3 * state_width), lambda f: (0, 0, 0)),
        ],
        out_specs=pl.BlockSpec((1, band, width, state_width), lambda f: (f, 0, 0, 0)),
        out_shape=jax.ShapeDtypeStruct((count, band, width, state_width), jnp.float32),
        scratch_shapes=[pltpu.VMEM((band * width, state_width), jnp.float32)],
        compiler_params=pltpu.CompilerParams(dimension_semantics=("arbitrary",)),
    )(decay, top, frames, bottom, grouped_taps(conv_in))


def output_stage(local, cumulative, incoming, frames, conv_out, skip):
    count, band, width, state_width = local.shape
    channels = conv_out.shape[3]
    edges = jnp.concatenate([local[:, :1], local[:, -1:]], axis=1)
    edges = edges + cumulative[:, None, None, :] * jnp.concatenate(
        [incoming[None, :1], incoming[None, -1:]], axis=1
    )
    top, bottom = halo_rows(edges.astype(jnp.bfloat16), "rows", 1)
    halo = pl.BlockSpec((1, 1, width, state_width), lambda f: (f, 0, 0, 0))
    return pl.pallas_call(
        output_kernel,
        grid=(count,),
        in_specs=[
            pl.BlockSpec((count, state_width), lambda f: (0, 0)),
            pl.BlockSpec((1, channels), lambda f: (0, 0)),
            pl.BlockSpec((band, width, state_width), lambda f: (0, 0, 0)),
            halo,
            pl.BlockSpec((1, band, width, state_width), lambda f: (f, 0, 0, 0)),
            halo,
            pl.BlockSpec((1, band, width, channels), lambda f: (f, 0, 0, 0)),
            pl.BlockSpec((3, state_width, 3 * channels), lambda f: (0, 0, 0)),
        ],
        out_specs=pl.BlockSpec((1, band, width, channels), lambda f: (f, 0, 0, 0)),
        out_shape=jax.ShapeDtypeStruct((count, band, width, channels), jnp.bfloat16),
        compiler_params=pltpu.CompilerParams(dimension_semantics=("arbitrary",)),
    )(cumulative, skip.reshape(1, channels), incoming, top, local, bottom, frames, grouped_taps(conv_out))


def incoming_state(products, state, axis):
    n = lax.axis_size(axis)
    me = lax.axis_index(axis)
    block = lax.broadcasted_iota(jnp.int32, (n, 1), 0)

    def span(lo, hi):
        inside = (block >= lo) & (block <= hi)
        return jnp.prod(jnp.where(inside, products, 1.0), axis=0)

    win_s = state
    acc_s = None
    shift = 1
    while shift < n:
        pairs = [(i, i + shift) for i in range(n - shift)]
        got = lax.ppermute(win_s.astype(jnp.bfloat16), axis, pairs).astype(jnp.float32)
        if acc_s is None:
            acc_s = got
        else:
            acc_s = span(me - shift + 1, me - 1) * got + acc_s
        if 2 * shift < n:
            win_s = span(me - shift + 1, me) * got + win_s
        shift *= 2
    if acc_s is None:
        return jnp.zeros_like(state)
    return acc_s


def shards(frames, conv_in, decay, conv_out, skip):
    with jax.named_scope("block_decay_products"):
        cumulative = jnp.cumprod(decay, axis=0)
        products = lax.all_gather(cumulative[-1], "tm")
    with jax.named_scope("input_conv_and_recurrence"):
        local = input_stage(frames, conv_in, decay)
    with jax.named_scope("carry_across_blocks"):
        incoming = incoming_state(products, local[-1], "tm")
    with jax.named_scope("output_conv"):
        return output_stage(local, cumulative, incoming, frames, conv_out, skip)


def solution(mesh):
    return jax.shard_map(
        shards,
        mesh=mesh,
        in_specs=(P("tm", "rows", None, None), P(), P("tm", None), P(), P()),
        out_specs=P("tm", "rows", None, None),
        check_vma=False,
    )
```

```python
import jax
import jax.numpy as jnp
from jax import lax
from jax.experimental import pallas as pl
from jax.experimental.pallas import tpu as pltpu
from jax.sharding import PartitionSpec as P


def halo_rows(x, axis, dim):
    size, length = (lax.axis_size(axis), x.shape[dim])
    up = [(i, (i + 1) % size) for i in range(size - 1)]
    down = [(j, i) for i, j in up]
    last = lax.slice_in_dim(x, length - 1, length, axis=dim)
    first = lax.slice_in_dim(x, 0, 1, axis=dim)
    before = lax.ppermute(last, axis, up)
    after = lax.ppermute(first, axis, down)
    return before, after


def conv_taps(x, w_ref):
    rows = x.shape[0] - 2
    width, k = x.shape[1], x.shape[2]
    m = w_ref.shape[3]
    n = rows * width
    lhs = jnp.concatenate([x[a : a + rows].reshape(n, k) for a in range(3)], axis=1)
    weight = jnp.concatenate(
        [jnp.concatenate([w_ref[a, b] for b in range(3)], axis=1) for a in range(3)], axis=0
    )
    acc = jnp.dot(lhs, weight, preferred_element_type=jnp.float32)
    column = lax.broadcasted_iota(jnp.int32, (n, m), 0) % width
    from_left = pltpu.roll(acc[:, :m], 1, 0)
    from_right = pltpu.roll(acc[:, 2 * m :], n - 1, 0)
    total = acc[:, m : 2 * m]
    total = total + jnp.where(column == 0, 0.0, from_left)
    total = total + jnp.where(column == width - 1, 0.0, from_right)
    return total


def input_kernel(decay_ref, top_ref, frame_ref, bottom_ref, w_ref, out_ref, state_ref):
    f = pl.program_id(0)
    band, width, m = out_ref.shape[1:]

    @pl.when(f == 0)
    def _():
        state_ref[...] = jnp.zeros_like(state_ref)

    x = jnp.concatenate([top_ref[0], frame_ref[0], bottom_ref[0]], axis=0)
    drive = conv_taps(x, w_ref)
    state = decay_ref[pl.ds(f, 1), :] * state_ref[...] + drive
    state_ref[...] = state
    out_ref[0] = state.reshape(band, width, m)


def output_kernel(
    cum_ref, skip_ref, incoming_ref, top_ref, local_ref, bottom_ref, frame_ref, w_ref, out_ref
):
    f = pl.program_id(0)
    band, width, m = out_ref.shape[1:]
    inner = (local_ref[0] + cum_ref[pl.ds(f, 1), :] * incoming_ref[...]).astype(jnp.bfloat16)
    x = jnp.concatenate([top_ref[0], inner, bottom_ref[0]], axis=0)
    total = conv_taps(x, w_ref)
    frame = frame_ref[0].reshape(band * width, m).astype(jnp.float32)
    total = total + skip_ref[...] * frame
    out_ref[0] = total.astype(jnp.bfloat16).reshape(band, width, m)


def input_stage(frames, conv_in, decay):
    count, band, width, channels = frames.shape
    state_width = conv_in.shape[3]
    top, bottom = halo_rows(frames, "rows", 1)
    halo = pl.BlockSpec((1, 1, width, channels), lambda f: (f, 0, 0, 0))
    return pl.pallas_call(
        input_kernel,
        grid=(count,),
        in_specs=[
            pl.BlockSpec((count, state_width), lambda f: (0, 0)),
            halo,
            pl.BlockSpec((1, band, width, channels), lambda f: (f, 0, 0, 0)),
            halo,
            pl.BlockSpec((3, 3, channels, state_width), lambda f: (0, 0, 0, 0)),
        ],
        out_specs=pl.BlockSpec((1, band, width, state_width), lambda f: (f, 0, 0, 0)),
        out_shape=jax.ShapeDtypeStruct((count, band, width, state_width), jnp.float32),
        scratch_shapes=[pltpu.VMEM((band * width, state_width), jnp.float32)],
        compiler_params=pltpu.CompilerParams(dimension_semantics=("arbitrary",)),
    )(decay, top, frames, bottom, conv_in)


def output_stage(local, cumulative, incoming, frames, conv_out, skip):
    count, band, width, state_width = local.shape
    channels = conv_out.shape[3]
    edges = jnp.concatenate([local[:, :1], local[:, -1:]], axis=1)
    edges = edges + cumulative[:, None, None, :] * jnp.concatenate(
        [incoming[None, :1], incoming[None, -1:]], axis=1
    )
    top, bottom = halo_rows(edges.astype(jnp.bfloat16), "rows", 1)
    halo = pl.BlockSpec((1, 1, width, state_width), lambda f: (f, 0, 0, 0))
    return pl.pallas_call(
        output_kernel,
        grid=(count,),
        in_specs=[
            pl.BlockSpec((count, state_width), lambda f: (0, 0)),
            pl.BlockSpec((1, channels), lambda f: (0, 0)),
            pl.BlockSpec((band, width, state_width), lambda f: (0, 0, 0)),
            halo,
            pl.BlockSpec((1, band, width, state_width), lambda f: (f, 0, 0, 0)),
            halo,
            pl.BlockSpec((1, band, width, channels), lambda f: (f, 0, 0, 0)),
            pl.BlockSpec((3, 3, state_width, channels), lambda f: (0, 0, 0, 0)),
        ],
        out_specs=pl.BlockSpec((1, band, width, channels), lambda f: (f, 0, 0, 0)),
        out_shape=jax.ShapeDtypeStruct((count, band, width, channels), jnp.bfloat16),
        compiler_params=pltpu.CompilerParams(dimension_semantics=("arbitrary",)),
    )(cumulative, skip.reshape(1, channels), incoming, top, local, bottom, frames, conv_out)


def split3(p, rows):
    hi = lax.reduce_precision(p, exponent_bits=8, mantissa_bits=7)
    rest = p - hi
    mid = lax.reduce_precision(rest, exponent_bits=8, mantissa_bits=7)
    low = rest - mid
    parts = jnp.stack([hi, mid, low]).astype(jnp.bfloat16)
    return jnp.pad(parts, ((0, rows - 3), (0, 0)))


def incoming_state(power, state, axis):
    n = lax.axis_size(axis)
    rows, width, channels = state.shape
    cells = rows * width
    win_p, win_s = power, state
    acc_p, acc_s = None, None
    shift = 1
    while shift < n:
        pairs = [(i, i + shift) for i in range(n - shift)]
        payload = jnp.concatenate(
            [win_s.astype(jnp.bfloat16).reshape(cells, channels), split3(win_p, 16)], axis=0
        )
        got = lax.ppermute(payload, axis, pairs)
        got_s = got[:cells].astype(jnp.float32).reshape(rows, width, channels)
        got_p = jnp.sum(got[cells : cells + 3].astype(jnp.float32), axis=0)
        if acc_s is None:
            acc_p, acc_s = got_p, got_s
        else:
            acc_s = acc_p * got_s + acc_s
            acc_p = got_p * acc_p
        if 2 * shift < n:
            win_s = win_p * got_s + win_s
            win_p = got_p * win_p
        shift *= 2
    if acc_s is None:
        return jnp.zeros_like(state)
    return acc_s


def shards(frames, conv_in, decay, conv_out, skip):
    with jax.named_scope("block_decay_products"):
        running = [decay[0]]
        for frame_index in range(1, decay.shape[0]):
            running.append(running[-1] * decay[frame_index])
        cumulative = jnp.stack(running)
    with jax.named_scope("input_conv_and_recurrence"):
        local = input_stage(frames, conv_in, decay)
    with jax.named_scope("carry_across_blocks"):
        incoming = incoming_state(cumulative[-1], local[-1], "tm")
    with jax.named_scope("output_conv"):
        return output_stage(local, cumulative, incoming, frames, conv_out, skip)


def solution(mesh):
    return jax.shard_map(
        shards,
        mesh=mesh,
        in_specs=(P("tm", "rows", None, None), P(), P("tm", None), P(), P()),
        out_specs=P("tm", "rows", None, None),
        check_vma=False,
    )
```

```python
import jax
import jax.numpy as jnp
from jax import lax
from jax.experimental import pallas as pl
from jax.experimental.pallas import tpu as pltpu
from jax.sharding import PartitionSpec as P


def halo_rows(x, axis, dim):
    size, length = (lax.axis_size(axis), x.shape[dim])
    up = [(i, (i + 1) % size) for i in range(size - 1)]
    down = [(j, i) for i, j in up]
    last = lax.slice_in_dim(x, length - 1, length, axis=dim)
    first = lax.slice_in_dim(x, 0, 1, axis=dim)
    before = lax.ppermute(last, axis, up)
    after = lax.ppermute(first, axis, down)
    return before, after


def shifted_sum(acc, width, m):
    n = acc.shape[0]
    column = lax.broadcasted_iota(jnp.int32, (n, m), 0) % width
    from_left = pltpu.roll(acc[:, :m], 1, 0)
    from_right = pltpu.roll(acc[:, 2 * m :], n - 1, 0)
    total = acc[:, m : 2 * m]
    total = total + jnp.where(column == 0, 0.0, from_left)
    total = total + jnp.where(column == width - 1, 0.0, from_right)
    return total


def tap_row(w_ref, a):
    return jnp.concatenate([w_ref[a, b] for b in range(3)], axis=1)


def conv_band(band_rows, w_ref):
    rows, width, k = band_rows.shape
    m = w_ref.shape[3]
    n = rows * width
    zero = jnp.zeros((1, width, k), band_rows.dtype)
    x = jnp.concatenate([zero, band_rows, zero], axis=0)
    lhs = jnp.concatenate([x[a : a + rows].reshape(n, k) for a in range(3)], axis=1)
    weight = jnp.concatenate([tap_row(w_ref, a) for a in range(3)], axis=0)
    acc = jnp.dot(lhs, weight, preferred_element_type=jnp.float32)
    return shifted_sum(acc, width, m)


def halo_effect(row, w_ref, a):
    width = row.shape[0]
    m = w_ref.shape[3]
    acc = jnp.dot(row, tap_row(w_ref, a), preferred_element_type=jnp.float32)
    return shifted_sum(acc, width, m)


def input_kernel(decay_ref, frame_ref, w_ref, out_ref, state_ref):
    f = pl.program_id(0)
    band, width, m = out_ref.shape[1:]

    @pl.when(f == 0)
    def _():
        state_ref[...] = jnp.zeros_like(state_ref)

    drive = conv_band(frame_ref[0], w_ref)
    state = decay_ref[pl.ds(f, 1), :] * state_ref[...] + drive
    state_ref[...] = state
    out_ref[0] = state.reshape(band, width, m)


def input_edge_kernel(decay_ref, top_ref, bottom_ref, w_ref, out_ref):
    count, _, width, m = out_ref.shape
    upper = jnp.zeros((width, m), jnp.float32)
    lower = jnp.zeros((width, m), jnp.float32)
    for f in range(count):
        rate = decay_ref[f : f + 1, :]
        upper = rate * upper + halo_effect(top_ref[f, 0], w_ref, 0)
        lower = rate * lower + halo_effect(bottom_ref[f, 0], w_ref, 2)
        out_ref[f, 0] = upper
        out_ref[f, 1] = lower


def with_edges(local, edges):
    return jnp.concatenate([local[:1] + edges[:1], local[1:-1], local[-1:] + edges[1:]], axis=0)


def output_kernel(
    cum_ref, skip_ref, incoming_ref, edge_ref, local_ref, frame_ref, w_ref, out_ref, rim_ref
):
    f = pl.program_id(0)
    band, width, m = out_ref.shape[1:]
    state = with_edges(local_ref[0], edge_ref[0])
    inner = (state + cum_ref[pl.ds(f, 1), :] * incoming_ref[...]).astype(jnp.bfloat16)
    total = conv_band(inner, w_ref)
    frame = frame_ref[0].reshape(band * width, m).astype(jnp.float32)
    total = total + skip_ref[...] * frame
    out_ref[0] = total.astype(jnp.bfloat16).reshape(band, width, m)
    rim_ref[0, 0] = total[:width]
    rim_ref[0, 1] = total[(band - 1) * width :]


def output_edge_kernel(rim_ref, top_ref, bottom_ref, w_ref, out_ref):
    count = rim_ref.shape[0]
    for f in range(count):
        out_ref[f, 0] = (rim_ref[f, 0] + halo_effect(top_ref[f, 0], w_ref, 0)).astype(jnp.bfloat16)
        out_ref[f, 1] = (rim_ref[f, 1] + halo_effect(bottom_ref[f, 0], w_ref, 2)).astype(
            jnp.bfloat16
        )


def whole(shape):
    return pl.BlockSpec(shape, lambda: (0,) * len(shape))


def input_stage(frames, conv_in, decay):
    count, band, width, channels = frames.shape
    state_width = conv_in.shape[3]
    top, bottom = halo_rows(frames, "rows", 1)
    local = pl.pallas_call(
        input_kernel,
        grid=(count,),
        in_specs=[
            pl.BlockSpec((count, state_width), lambda f: (0, 0)),
            pl.BlockSpec((1, band, width, channels), lambda f: (f, 0, 0, 0)),
            pl.BlockSpec((3, 3, channels, state_width), lambda f: (0, 0, 0, 0)),
        ],
        out_specs=pl.BlockSpec((1, band, width, state_width), lambda f: (f, 0, 0, 0)),
        out_shape=jax.ShapeDtypeStruct((count, band, width, state_width), jnp.float32),
        scratch_shapes=[pltpu.VMEM((band * width, state_width), jnp.float32)],
        compiler_params=pltpu.CompilerParams(dimension_semantics=("arbitrary",)),
    )(decay, frames, conv_in)
    edges = pl.pallas_call(
        input_edge_kernel,
        in_specs=[
            whole(decay.shape),
            whole(top.shape),
            whole(bottom.shape),
            whole(conv_in.shape),
        ],
        out_specs=whole((count, 2, width, state_width)),
        out_shape=jax.ShapeDtypeStruct((count, 2, width, state_width), jnp.float32),
    )(decay, top, bottom, conv_in)
    return local, edges


def output_stage(local, edges, cumulative, incoming, frames, conv_out, skip):
    count, band, width, state_width = local.shape
    channels = conv_out.shape[3]
    rims = jnp.concatenate([local[:, :1], local[:, -1:]], axis=1) + edges
    rims = rims + cumulative[:, None, None, :] * jnp.concatenate(
        [incoming[None, :1], incoming[None, -1:]], axis=1
    )
    top, bottom = halo_rows(rims.astype(jnp.bfloat16), "rows", 1)
    body, rim = pl.pallas_call(
        output_kernel,
        grid=(count,),
        in_specs=[
            pl.BlockSpec((count, state_width), lambda f: (0, 0)),
            pl.BlockSpec((1, channels), lambda f: (0, 0)),
            pl.BlockSpec((band, width, state_width), lambda f: (0, 0, 0)),
            pl.BlockSpec((1, 2, width, state_width), lambda f: (f, 0, 0, 0)),
            pl.BlockSpec((1, band, width, state_width), lambda f: (f, 0, 0, 0)),
            pl.BlockSpec((1, band, width, channels), lambda f: (f, 0, 0, 0)),
            pl.BlockSpec((3, 3, state_width, channels), lambda f: (0, 0, 0, 0)),
        ],
        out_specs=[
            pl.BlockSpec((1, band, width, channels), lambda f: (f, 0, 0, 0)),
            pl.BlockSpec((1, 2, width, channels), lambda f: (f, 0, 0, 0)),
        ],
        out_shape=[
            jax.ShapeDtypeStruct((count, band, width, channels), jnp.bfloat16),
            jax.ShapeDtypeStruct((count, 2, width, channels), jnp.float32),
        ],
        compiler_params=pltpu.CompilerParams(dimension_semantics=("arbitrary",)),
    )(cumulative, skip.reshape(1, channels), incoming, edges, local, frames, conv_out)
    fixed = pl.pallas_call(
        output_edge_kernel,
        in_specs=[whole(rim.shape), whole(top.shape), whole(bottom.shape), whole(conv_out.shape)],
        out_specs=whole((count, 2, width, channels)),
        out_shape=jax.ShapeDtypeStruct((count, 2, width, channels), jnp.bfloat16),
    )(rim, top, bottom, conv_out)
    return body.at[:, :1].set(fixed[:, :1]).at[:, -1:].set(fixed[:, 1:])


def split3(p, rows):
    hi = lax.reduce_precision(p, exponent_bits=8, mantissa_bits=7)
    rest = p - hi
    mid = lax.reduce_precision(rest, exponent_bits=8, mantissa_bits=7)
    low = rest - mid
    parts = jnp.stack([hi, mid, low]).astype(jnp.bfloat16)
    return jnp.pad(parts, ((0, rows - 3), (0, 0)))


def incoming_state(power, state, axis):
    n = lax.axis_size(axis)
    rows, width, channels = state.shape
    cells = rows * width
    win_p, win_s = power, state
    acc_p, acc_s = None, None
    shift = 1
    while shift < n:
        pairs = [(i, i + shift) for i in range(n - shift)]
        payload = jnp.concatenate(
            [win_s.astype(jnp.bfloat16).reshape(cells, channels), split3(win_p, 16)], axis=0
        )
        got = lax.ppermute(payload, axis, pairs)
        got_s = got[:cells].astype(jnp.float32).reshape(rows, width, channels)
        got_p = jnp.sum(got[cells : cells + 3].astype(jnp.float32), axis=0)
        if acc_s is None:
            acc_p, acc_s = got_p, got_s
        else:
            acc_s = acc_p * got_s + acc_s
            acc_p = got_p * acc_p
        if 2 * shift < n:
            win_s = win_p * got_s + win_s
            win_p = got_p * win_p
        shift *= 2
    if acc_s is None:
        return jnp.zeros_like(state)
    return acc_s


def shards(frames, conv_in, decay, conv_out, skip):
    with jax.named_scope("block_decay_products"):
        running = [decay[0]]
        for frame_index in range(1, decay.shape[0]):
            running.append(running[-1] * decay[frame_index])
        cumulative = jnp.stack(running)
    with jax.named_scope("input_conv_and_recurrence"):
        local, edges = input_stage(frames, conv_in, decay)
    with jax.named_scope("carry_across_blocks"):
        incoming = incoming_state(cumulative[-1], with_edges(local[-1], edges[-1]), "tm")
    with jax.named_scope("output_conv"):
        return output_stage(local, edges, cumulative, incoming, frames, conv_out, skip)


def solution(mesh):
    return jax.shard_map(
        shards,
        mesh=mesh,
        in_specs=(P("tm", "rows", None, None), P(), P("tm", None), P(), P()),
        out_specs=P("tm", "rows", None, None),
        check_vma=False,
    )
```

```python
import jax
import jax.numpy as jnp
from jax import lax
from jax.experimental import pallas as pl
from jax.experimental.pallas import tpu as pltpu
from jax.sharding import PartitionSpec as P


def halo_rows(x, axis, dim):
    size, length = (lax.axis_size(axis), x.shape[dim])
    if size == 2:
        upper = lax.axis_index(axis) == 0
        last = lax.slice_in_dim(x, length - 1, length, axis=dim)
        first = lax.slice_in_dim(x, 0, 1, axis=dim)
        got = lax.ppermute(jnp.where(upper, last, first), axis, [(0, 1), (1, 0)])
        zero = jnp.zeros_like(got)
        return jnp.where(upper, zero, got), jnp.where(upper, got, zero)
    up = [(i, (i + 1) % size) for i in range(size - 1)]
    down = [(j, i) for i, j in up]
    last = lax.slice_in_dim(x, length - 1, length, axis=dim)
    first = lax.slice_in_dim(x, 0, 1, axis=dim)
    before = lax.ppermute(last, axis, up)
    after = lax.ppermute(first, axis, down)
    return before, after


def conv_taps(x, w_ref):
    rows = x.shape[0] - 2
    width, k = x.shape[1], x.shape[2]
    m = w_ref.shape[3]
    n = rows * width
    lhs = jnp.concatenate([x[a : a + rows].reshape(n, k) for a in range(3)], axis=1)
    weight = jnp.concatenate(
        [jnp.concatenate([w_ref[a, b] for b in range(3)], axis=1) for a in range(3)], axis=0
    )
    acc = jnp.dot(lhs, weight, preferred_element_type=jnp.float32)
    column = lax.broadcasted_iota(jnp.int32, (n, m), 0) % width
    from_left = pltpu.roll(acc[:, :m], 1, 0)
    from_right = pltpu.roll(acc[:, 2 * m :], n - 1, 0)
    total = acc[:, m : 2 * m]
    total = total + jnp.where(column == 0, 0.0, from_left)
    total = total + jnp.where(column == width - 1, 0.0, from_right)
    return total


def input_kernel(
    decay_ref, top_ref, frame_ref, bottom_ref, w_ref, out_ref, cum_ref, send_ref, state_ref, power_ref
):
    f = pl.program_id(0)
    band, width, m = out_ref.shape[1:]
    cells = band * width

    @pl.when(f == 0)
    def _():
        state_ref[...] = jnp.zeros_like(state_ref)
        power_ref[...] = jnp.ones_like(power_ref)

    x = jnp.concatenate([top_ref[0], frame_ref[0], bottom_ref[0]], axis=0)
    drive = conv_taps(x, w_ref)
    rate = decay_ref[pl.ds(f, 1), :]
    state = rate * state_ref[...] + drive
    power = rate * power_ref[...]
    state_ref[...] = state
    power_ref[...] = power
    out_ref[0] = state.reshape(band, width, m)
    cum_ref[pl.ds(f, 1), :] = power

    @pl.when(f == pl.num_programs(0) - 1)
    def _():
        hi = power.astype(jnp.bfloat16)
        rest = power - hi.astype(jnp.float32)
        mid = rest.astype(jnp.bfloat16)
        low = (rest - mid.astype(jnp.float32)).astype(jnp.bfloat16)
        pad = send_ref.shape[0] - cells - 3
        send_ref[...] = jnp.concatenate(
            [state.astype(jnp.bfloat16), hi, mid, low, jnp.zeros((pad, m), jnp.bfloat16)], axis=0
        )


def output_kernel(
    cum_ref, skip_ref, incoming_ref, top_ref, local_ref, bottom_ref, frame_ref, w_ref, out_ref
):
    f = pl.program_id(0)
    band, width, m = out_ref.shape[1:]
    inner = (local_ref[0] + cum_ref[pl.ds(f, 1), :] * incoming_ref[...]).astype(jnp.bfloat16)
    x = jnp.concatenate([top_ref[0], inner, bottom_ref[0]], axis=0)
    total = conv_taps(x, w_ref)
    frame = frame_ref[0].reshape(band * width, m).astype(jnp.float32)
    total = total + skip_ref[...] * frame
    out_ref[0] = total.astype(jnp.bfloat16).reshape(band, width, m)


def input_stage(frames, conv_in, decay):
    count, band, width, channels = frames.shape
    state_width = conv_in.shape[3]
    top, bottom = halo_rows(frames, "rows", 1)
    halo = pl.BlockSpec((1, 1, width, channels), lambda f: (f, 0, 0, 0))
    payload_rows = band * width + 16
    return pl.pallas_call(
        input_kernel,
        grid=(count,),
        in_specs=[
            pl.BlockSpec((count, state_width), lambda f: (0, 0)),
            halo,
            pl.BlockSpec((1, band, width, channels), lambda f: (f, 0, 0, 0)),
            halo,
            pl.BlockSpec((3, 3, channels, state_width), lambda f: (0, 0, 0, 0)),
        ],
        out_specs=[
            pl.BlockSpec((1, band, width, state_width), lambda f: (f, 0, 0, 0)),
            pl.BlockSpec((count, state_width), lambda f: (0, 0)),
            pl.BlockSpec((payload_rows, state_width), lambda f: (0, 0)),
        ],
        out_shape=[
            jax.ShapeDtypeStruct((count, band, width, state_width), jnp.float32),
            jax.ShapeDtypeStruct((count, state_width), jnp.float32),
            jax.ShapeDtypeStruct((payload_rows, state_width), jnp.bfloat16),
        ],
        scratch_shapes=[
            pltpu.VMEM((band * width, state_width), jnp.float32),
            pltpu.VMEM((1, state_width), jnp.float32),
        ],
        compiler_params=pltpu.CompilerParams(dimension_semantics=("arbitrary",)),
    )(decay, top, frames, bottom, conv_in)


def output_stage(local, cumulative, incoming, frames, conv_out, skip):
    count, band, width, state_width = local.shape
    channels = conv_out.shape[3]
    edges = jnp.concatenate([local[:, :1], local[:, -1:]], axis=1)
    edges = edges + cumulative[:, None, None, :] * jnp.concatenate(
        [incoming[None, :1], incoming[None, -1:]], axis=1
    )
    top, bottom = halo_rows(edges.astype(jnp.bfloat16), "rows", 1)
    halo = pl.BlockSpec((1, 1, width, state_width), lambda f: (f, 0, 0, 0))
    return pl.pallas_call(
        output_kernel,
        grid=(count,),
        in_specs=[
            pl.BlockSpec((count, state_width), lambda f: (0, 0)),
            pl.BlockSpec((1, channels), lambda f: (0, 0)),
            pl.BlockSpec((band, width, state_width), lambda f: (0, 0, 0)),
            halo,
            pl.BlockSpec((1, band, width, state_width), lambda f: (f, 0, 0, 0)),
            halo,
            pl.BlockSpec((1, band, width, channels), lambda f: (f, 0, 0, 0)),
            pl.BlockSpec((3, 3, state_width, channels), lambda f: (0, 0, 0, 0)),
        ],
        out_specs=pl.BlockSpec((1, band, width, channels), lambda f: (f, 0, 0, 0)),
        out_shape=jax.ShapeDtypeStruct((count, band, width, channels), jnp.bfloat16),
        compiler_params=pltpu.CompilerParams(dimension_semantics=("arbitrary",)),
    )(cumulative, skip.reshape(1, channels), incoming, top, local, bottom, frames, conv_out)


def split3(p, rows):
    hi = lax.reduce_precision(p, exponent_bits=8, mantissa_bits=7)
    rest = p - hi
    mid = lax.reduce_precision(rest, exponent_bits=8, mantissa_bits=7)
    low = rest - mid
    parts = jnp.stack([hi, mid, low]).astype(jnp.bfloat16)
    return jnp.pad(parts, ((0, rows - 3), (0, 0)))


def incoming_state(power, state, first_payload, axis):
    n = lax.axis_size(axis)
    rows, width, channels = state.shape
    cells = rows * width
    win_p, win_s = power, state
    acc_p, acc_s = None, None
    payload = first_payload
    shift = 1
    while shift < n:
        pairs = [(i, i + shift) for i in range(n - shift)]
        if payload is None:
            payload = jnp.concatenate(
                [win_s.astype(jnp.bfloat16).reshape(cells, channels), split3(win_p, 16)], axis=0
            )
        got = lax.ppermute(payload, axis, pairs)
        payload = None
        got_s = got[:cells].astype(jnp.float32).reshape(rows, width, channels)
        got_p = jnp.sum(got[cells : cells + 3].astype(jnp.float32), axis=0)
        if acc_s is None:
            acc_p, acc_s = got_p, got_s
        else:
            acc_s = acc_p * got_s + acc_s
            acc_p = got_p * acc_p
        if 2 * shift < n:
            win_s = win_p * got_s + win_s
            win_p = got_p * win_p
        shift *= 2
    if acc_s is None:
        return jnp.zeros_like(state)
    return acc_s


def shards(frames, conv_in, decay, conv_out, skip):
    with jax.named_scope("input_conv_and_recurrence"):
        local, cumulative, first_payload = input_stage(frames, conv_in, decay)
    with jax.named_scope("carry_across_blocks"):
        incoming = incoming_state(cumulative[-1], local[-1], first_payload, "tm")
    with jax.named_scope("output_conv"):
        return output_stage(local, cumulative, incoming, frames, conv_out, skip)


def solution(mesh):
    return jax.shard_map(
        shards,
        mesh=mesh,
        in_specs=(P("tm", "rows", None, None), P(), P("tm", None), P(), P()),
        out_specs=P("tm", "rows", None, None),
        check_vma=False,
    )
```

```python
import jax
import jax.numpy as jnp
from jax import lax
from jax.experimental import pallas as pl
from jax.experimental.pallas import tpu as pltpu
from jax.sharding import PartitionSpec as P

CHUNKS = 2


def halo_rows(x, axis, dim):
    size, length = (lax.axis_size(axis), x.shape[dim])
    if size == 2:
        upper = lax.axis_index(axis) == 0
        last = lax.slice_in_dim(x, length - 1, length, axis=dim)
        first = lax.slice_in_dim(x, 0, 1, axis=dim)
        got = lax.ppermute(jnp.where(upper, last, first), axis, [(0, 1), (1, 0)])
        zero = jnp.zeros_like(got)
        return jnp.where(upper, zero, got), jnp.where(upper, got, zero)
    up = [(i, (i + 1) % size) for i in range(size - 1)]
    down = [(j, i) for i, j in up]
    last = lax.slice_in_dim(x, length - 1, length, axis=dim)
    first = lax.slice_in_dim(x, 0, 1, axis=dim)
    before = lax.ppermute(last, axis, up)
    after = lax.ppermute(first, axis, down)
    return before, after


def conv_taps(x, w_ref):
    rows = x.shape[0] - 2
    width, k = x.shape[1], x.shape[2]
    m = w_ref.shape[3]
    n = rows * width
    lhs = jnp.concatenate([x[a : a + rows].reshape(n, k) for a in range(3)], axis=1)
    weight = jnp.concatenate(
        [jnp.concatenate([w_ref[a, b] for b in range(3)], axis=1) for a in range(3)], axis=0
    )
    acc = jnp.dot(lhs, weight, preferred_element_type=jnp.float32)
    column = lax.broadcasted_iota(jnp.int32, (n, m), 0) % width
    from_left = pltpu.roll(acc[:, :m], 1, 0)
    from_right = pltpu.roll(acc[:, 2 * m :], n - 1, 0)
    total = acc[:, m : 2 * m]
    total = total + jnp.where(column == 0, 0.0, from_left)
    total = total + jnp.where(column == width - 1, 0.0, from_right)
    return total


def input_kernel(
    decay_ref, top_ref, frame_ref, bottom_ref, w_ref, out_ref, cum_ref, send_ref, state_ref, power_ref
):
    f = pl.program_id(0)
    band, width, m = out_ref.shape[1:]
    cells = band * width

    @pl.when(f == 0)
    def _():
        state_ref[...] = jnp.zeros_like(state_ref)
        power_ref[...] = jnp.ones_like(power_ref)

    x = jnp.concatenate([top_ref[0], frame_ref[0], bottom_ref[0]], axis=0)
    drive = conv_taps(x, w_ref)
    rate = decay_ref[pl.ds(f, 1), :]
    state = rate * state_ref[...] + drive
    power = rate * power_ref[...]
    state_ref[...] = state
    power_ref[...] = power
    out_ref[0] = state.reshape(band, width, m)
    cum_ref[pl.ds(f, 1), :] = power

    @pl.when(f == pl.num_programs(0) - 1)
    def _():
        hi = power.astype(jnp.bfloat16)
        rest = power - hi.astype(jnp.float32)
        mid = rest.astype(jnp.bfloat16)
        low = (rest - mid.astype(jnp.float32)).astype(jnp.bfloat16)
        chunks, chunk_rows = send_ref.shape[0], send_ref.shape[1]
        part = cells // chunks
        pad = jnp.zeros((chunk_rows - part - 3, m), jnp.bfloat16)
        for c in range(chunks):
            piece = state[c * part : (c + 1) * part].astype(jnp.bfloat16)
            send_ref[c] = jnp.concatenate([piece, hi, mid, low, pad], axis=0)


def output_kernel(
    cum_ref, skip_ref, incoming_ref, top_ref, local_ref, bottom_ref, frame_ref, w_ref, out_ref
):
    f = pl.program_id(0)
    band, width, m = out_ref.shape[1:]
    inner = (local_ref[0] + cum_ref[pl.ds(f, 1), :] * incoming_ref[...]).astype(jnp.bfloat16)
    x = jnp.concatenate([top_ref[0], inner, bottom_ref[0]], axis=0)
    total = conv_taps(x, w_ref)
    frame = frame_ref[0].reshape(band * width, m).astype(jnp.float32)
    total = total + skip_ref[...] * frame
    out_ref[0] = total.astype(jnp.bfloat16).reshape(band, width, m)


def input_stage(frames, conv_in, decay):
    count, band, width, channels = frames.shape
    state_width = conv_in.shape[3]
    top, bottom = halo_rows(frames, "rows", 1)
    halo = pl.BlockSpec((1, 1, width, channels), lambda f: (f, 0, 0, 0))
    payload_shape = (CHUNKS, band * width // CHUNKS + 16, state_width)
    return pl.pallas_call(
        input_kernel,
        grid=(count,),
        in_specs=[
            pl.BlockSpec((count, state_width), lambda f: (0, 0)),
            halo,
            pl.BlockSpec((1, band, width, channels), lambda f: (f, 0, 0, 0)),
            halo,
            pl.BlockSpec((3, 3, channels, state_width), lambda f: (0, 0, 0, 0)),
        ],
        out_specs=[
            pl.BlockSpec((1, band, width, state_width), lambda f: (f, 0, 0, 0)),
            pl.BlockSpec((count, state_width), lambda f: (0, 0)),
            pl.BlockSpec(payload_shape, lambda f: (0, 0, 0)),
        ],
        out_shape=[
            jax.ShapeDtypeStruct((count, band, width, state_width), jnp.float32),
            jax.ShapeDtypeStruct((count, state_width), jnp.float32),
            jax.ShapeDtypeStruct(payload_shape, jnp.bfloat16),
        ],
        scratch_shapes=[
            pltpu.VMEM((band * width, state_width), jnp.float32),
            pltpu.VMEM((1, state_width), jnp.float32),
        ],
        compiler_params=pltpu.CompilerParams(dimension_semantics=("arbitrary",)),
    )(decay, top, frames, bottom, conv_in)


def output_stage(local, cumulative, incoming, frames, conv_out, skip):
    count, band, width, state_width = local.shape
    channels = conv_out.shape[3]
    edges = jnp.concatenate([local[:, :1], local[:, -1:]], axis=1)
    edges = edges + cumulative[:, None, None, :] * jnp.concatenate(
        [incoming[None, :1], incoming[None, -1:]], axis=1
    )
    top, bottom = halo_rows(edges.astype(jnp.bfloat16), "rows", 1)
    halo = pl.BlockSpec((1, 1, width, state_width), lambda f: (f, 0, 0, 0))
    return pl.pallas_call(
        output_kernel,
        grid=(count,),
        in_specs=[
            pl.BlockSpec((count, state_width), lambda f: (0, 0)),
            pl.BlockSpec((1, channels), lambda f: (0, 0)),
            pl.BlockSpec((band, width, state_width), lambda f: (0, 0, 0)),
            halo,
            pl.BlockSpec((1, band, width, state_width), lambda f: (f, 0, 0, 0)),
            halo,
            pl.BlockSpec((1, band, width, channels), lambda f: (f, 0, 0, 0)),
            pl.BlockSpec((3, 3, state_width, channels), lambda f: (0, 0, 0, 0)),
        ],
        out_specs=pl.BlockSpec((1, band, width, channels), lambda f: (f, 0, 0, 0)),
        out_shape=jax.ShapeDtypeStruct((count, band, width, channels), jnp.bfloat16),
        compiler_params=pltpu.CompilerParams(dimension_semantics=("arbitrary",)),
    )(cumulative, skip.reshape(1, channels), incoming, top, local, bottom, frames, conv_out)


def split3(p, rows):
    hi = lax.reduce_precision(p, exponent_bits=8, mantissa_bits=7)
    rest = p - hi
    mid = lax.reduce_precision(rest, exponent_bits=8, mantissa_bits=7)
    low = rest - mid
    parts = jnp.stack([hi, mid, low]).astype(jnp.bfloat16)
    return jnp.pad(parts, ((0, rows - 3), (0, 0)))


def incoming_state(power, state, first_payload, axis):
    n = lax.axis_size(axis)
    cells, channels = state.shape
    win_p, win_s = power, state
    acc_p, acc_s = None, None
    payload = first_payload
    shift = 1
    while shift < n:
        pairs = [(i, i + shift) for i in range(n - shift)]
        if payload is None:
            payload = jnp.concatenate(
                [win_s.astype(jnp.bfloat16), split3(win_p, 16)], axis=0
            )
        got = lax.ppermute(payload, axis, pairs)
        payload = None
        got_s = got[:cells].astype(jnp.float32)
        got_p = jnp.sum(got[cells : cells + 3].astype(jnp.float32), axis=0)
        if acc_s is None:
            acc_p, acc_s = got_p, got_s
        else:
            acc_s = acc_p * got_s + acc_s
            acc_p = got_p * acc_p
        if 2 * shift < n:
            win_s = win_p * got_s + win_s
            win_p = got_p * win_p
        shift *= 2
    if acc_s is None:
        return jnp.zeros_like(state)
    return acc_s


def shards(frames, conv_in, decay, conv_out, skip):
    with jax.named_scope("input_conv_and_recurrence"):
        local, cumulative, first_payload = input_stage(frames, conv_in, decay)
    with jax.named_scope("carry_across_blocks"):
        count, band, width, state_width = local.shape
        end = local[-1].reshape(band * width, state_width)
        part = band * width // CHUNKS
        pieces = [
            incoming_state(cumulative[-1], end[c * part : (c + 1) * part], first_payload[c], "tm")
            for c in range(CHUNKS)
        ]
        incoming = jnp.concatenate(pieces, axis=0).reshape(band, width, state_width)
    with jax.named_scope("output_conv"):
        return output_stage(local, cumulative, incoming, frames, conv_out, skip)


def solution(mesh):
    return jax.shard_map(
        shards,
        mesh=mesh,
        in_specs=(P("tm", "rows", None, None), P(), P("tm", None), P(), P()),
        out_specs=P("tm", "rows", None, None),
        check_vma=False,
    )
```

```python
import jax
import jax.numpy as jnp
from jax import lax
from jax.experimental import pallas as pl
from jax.experimental.pallas import tpu as pltpu
from jax.sharding import PartitionSpec as P


def halo_rows(x, axis, dim):
    size, length = (lax.axis_size(axis), x.shape[dim])
    position = lax.axis_index(axis)
    if size == 2:
        row = (1 - position) * (length - 1)
        got = lax.ppermute(lax.dynamic_slice_in_dim(x, row, 1, axis=dim), axis, [(0, 1), (1, 0)])
        flags = jnp.stack([position == 1, position == 0]).astype(jnp.int32)
        return got, got, flags
    up = [(i, (i + 1) % size) for i in range(size - 1)]
    down = [(j, i) for i, j in up]
    last = lax.slice_in_dim(x, length - 1, length, axis=dim)
    first = lax.slice_in_dim(x, 0, 1, axis=dim)
    before = lax.ppermute(last, axis, up)
    after = lax.ppermute(first, axis, down)
    return before, after, jnp.ones((2,), jnp.int32)


def padded_band(flags_ref, above, band_rows, below):
    zero = jnp.zeros_like(above)
    top = jnp.where(flags_ref[0] == 1, above, zero)
    bottom = jnp.where(flags_ref[1] == 1, below, zero)
    return jnp.concatenate([top, band_rows, bottom], axis=0)


def conv_taps(x, w_ref):
    rows = x.shape[0] - 2
    width, k = x.shape[1], x.shape[2]
    m = w_ref.shape[3]
    n = rows * width
    lhs = jnp.concatenate([x[a : a + rows].reshape(n, k) for a in range(3)], axis=1)
    weight = jnp.concatenate(
        [jnp.concatenate([w_ref[a, b] for b in range(3)], axis=1) for a in range(3)], axis=0
    )
    acc = jnp.dot(lhs, weight, preferred_element_type=jnp.float32)
    column = lax.broadcasted_iota(jnp.int32, (n, m), 0) % width
    from_left = pltpu.roll(acc[:, :m], 1, 0)
    from_right = pltpu.roll(acc[:, 2 * m :], n - 1, 0)
    total = acc[:, m : 2 * m]
    total = total + jnp.where(column == 0, 0.0, from_left)
    total = total + jnp.where(column == width - 1, 0.0, from_right)
    return total


def input_kernel(
    flags_ref,
    decay_ref,
    top_ref,
    frame_ref,
    bottom_ref,
    w_ref,
    out_ref,
    cum_ref,
    send_ref,
    state_ref,
    power_ref,
):
    f = pl.program_id(0)
    band, width, m = out_ref.shape[1:]
    cells = band * width

    @pl.when(f == 0)
    def _():
        state_ref[...] = jnp.zeros_like(state_ref)
        power_ref[...] = jnp.ones_like(power_ref)

    x = padded_band(flags_ref, top_ref[0], frame_ref[0], bottom_ref[0])
    drive = conv_taps(x, w_ref)
    rate = decay_ref[pl.ds(f, 1), :]
    state = rate * state_ref[...] + drive
    power = rate * power_ref[...]
    state_ref[...] = state
    power_ref[...] = power
    out_ref[0] = state.reshape(band, width, m)
    cum_ref[pl.ds(f, 1), :] = power

    @pl.when(f == pl.num_programs(0) - 1)
    def _():
        hi = power.astype(jnp.bfloat16)
        rest = power - hi.astype(jnp.float32)
        mid = rest.astype(jnp.bfloat16)
        low = (rest - mid.astype(jnp.float32)).astype(jnp.bfloat16)
        pad = send_ref.shape[0] - cells - 3
        send_ref[...] = jnp.concatenate(
            [state.astype(jnp.bfloat16), hi, mid, low, jnp.zeros((pad, m), jnp.bfloat16)], axis=0
        )


def output_kernel(
    flags_ref, cum_ref, skip_ref, incoming_ref, top_ref, local_ref, bottom_ref, frame_ref, w_ref, out_ref
):
    f = pl.program_id(0)
    band, width, m = out_ref.shape[1:]
    inner = (local_ref[0] + cum_ref[pl.ds(f, 1), :] * incoming_ref[...]).astype(jnp.bfloat16)
    x = padded_band(flags_ref, top_ref[0], inner, bottom_ref[0])
    total = conv_taps(x, w_ref)
    frame = frame_ref[0].reshape(band * width, m).astype(jnp.float32)
    total = total + skip_ref[...] * frame
    out_ref[0] = total.astype(jnp.bfloat16).reshape(band, width, m)


def input_stage(frames, conv_in, decay):
    count, band, width, channels = frames.shape
    state_width = conv_in.shape[3]
    top, bottom, flags = halo_rows(frames, "rows", 1)
    halo = pl.BlockSpec((1, 1, width, channels), lambda f: (f, 0, 0, 0))
    payload_rows = band * width + 16
    return pl.pallas_call(
        input_kernel,
        grid=(count,),
        in_specs=[
            pl.BlockSpec(memory_space=pltpu.SMEM),
            pl.BlockSpec((count, state_width), lambda f: (0, 0)),
            halo,
            pl.BlockSpec((1, band, width, channels), lambda f: (f, 0, 0, 0)),
            halo,
            pl.BlockSpec((3, 3, channels, state_width), lambda f: (0, 0, 0, 0)),
        ],
        out_specs=[
            pl.BlockSpec((1, band, width, state_width), lambda f: (f, 0, 0, 0)),
            pl.BlockSpec((count, state_width), lambda f: (0, 0)),
            pl.BlockSpec((payload_rows, state_width), lambda f: (0, 0)),
        ],
        out_shape=[
            jax.ShapeDtypeStruct((count, band, width, state_width), jnp.float32),
            jax.ShapeDtypeStruct((count, state_width), jnp.float32),
            jax.ShapeDtypeStruct((payload_rows, state_width), jnp.bfloat16),
        ],
        scratch_shapes=[
            pltpu.VMEM((band * width, state_width), jnp.float32),
            pltpu.VMEM((1, state_width), jnp.float32),
        ],
        compiler_params=pltpu.CompilerParams(dimension_semantics=("arbitrary",)),
    )(flags, decay, top, frames, bottom, conv_in)


def output_stage(local, cumulative, incoming, frames, conv_out, skip):
    count, band, width, state_width = local.shape
    channels = conv_out.shape[3]
    edges = jnp.concatenate([local[:, :1], local[:, -1:]], axis=1)
    edges = edges + cumulative[:, None, None, :] * jnp.concatenate(
        [incoming[None, :1], incoming[None, -1:]], axis=1
    )
    top, bottom, flags = halo_rows(edges.astype(jnp.bfloat16), "rows", 1)
    halo = pl.BlockSpec((1, 1, width, state_width), lambda f: (f, 0, 0, 0))
    return pl.pallas_call(
        output_kernel,
        grid=(count,),
        in_specs=[
            pl.BlockSpec(memory_space=pltpu.SMEM),
            pl.BlockSpec((count, state_width), lambda f: (0, 0)),
            pl.BlockSpec((1, channels), lambda f: (0, 0)),
            pl.BlockSpec((band, width, state_width), lambda f: (0, 0, 0)),
            halo,
            pl.BlockSpec((1, band, width, state_width), lambda f: (f, 0, 0, 0)),
            halo,
            pl.BlockSpec((1, band, width, channels), lambda f: (f, 0, 0, 0)),
            pl.BlockSpec((3, 3, state_width, channels), lambda f: (0, 0, 0, 0)),
        ],
        out_specs=pl.BlockSpec((1, band, width, channels), lambda f: (f, 0, 0, 0)),
        out_shape=jax.ShapeDtypeStruct((count, band, width, channels), jnp.bfloat16),
        compiler_params=pltpu.CompilerParams(dimension_semantics=("arbitrary",)),
    )(flags, cumulative, skip.reshape(1, channels), incoming, top, local, bottom, frames, conv_out)


def split3(p, rows):
    hi = lax.reduce_precision(p, exponent_bits=8, mantissa_bits=7)
    rest = p - hi
    mid = lax.reduce_precision(rest, exponent_bits=8, mantissa_bits=7)
    low = rest - mid
    parts = jnp.stack([hi, mid, low]).astype(jnp.bfloat16)
    return jnp.pad(parts, ((0, rows - 3), (0, 0)))


def incoming_state(power, state, first_payload, axis):
    n = lax.axis_size(axis)
    rows, width, channels = state.shape
    cells = rows * width
    win_p, win_s = power, state
    acc_p, acc_s = None, None
    payload = first_payload
    shift = 1
    while shift < n:
        pairs = [(i, i + shift) for i in range(n - shift)]
        if payload is None:
            payload = jnp.concatenate(
                [win_s.astype(jnp.bfloat16).reshape(cells, channels), split3(win_p, 16)], axis=0
            )
        got = lax.ppermute(payload, axis, pairs)
        payload = None
        got_s = got[:cells].astype(jnp.float32).reshape(rows, width, channels)
        got_p = jnp.sum(got[cells : cells + 3].astype(jnp.float32), axis=0)
        if acc_s is None:
            acc_p, acc_s = got_p, got_s
        else:
            acc_s = acc_p * got_s + acc_s
            acc_p = got_p * acc_p
        if 2 * shift < n:
            win_s = win_p * got_s + win_s
            win_p = got_p * win_p
        shift *= 2
    if acc_s is None:
        return jnp.zeros_like(state)
    return acc_s


def shards(frames, conv_in, decay, conv_out, skip):
    with jax.named_scope("input_conv_and_recurrence"):
        local, cumulative, first_payload = input_stage(frames, conv_in, decay)
    with jax.named_scope("carry_across_blocks"):
        incoming = incoming_state(cumulative[-1], local[-1], first_payload, "tm")
    with jax.named_scope("output_conv"):
        return output_stage(local, cumulative, incoming, frames, conv_out, skip)


def solution(mesh):
    return jax.shard_map(
        shards,
        mesh=mesh,
        in_specs=(P("tm", "rows", None, None), P(), P("tm", None), P(), P()),
        out_specs=P("tm", "rows", None, None),
        check_vma=False,
    )
```

```python
import jax
import jax.numpy as jnp
from jax import lax
from jax.experimental import pallas as pl
from jax.experimental.pallas import tpu as pltpu
from jax.sharding import PartitionSpec as P


def halo_rows(x, axis, dim):
    size, length = (lax.axis_size(axis), x.shape[dim])
    if size == 2:
        row = (1 - lax.axis_index(axis)) * (length - 1)
        got = lax.ppermute(lax.dynamic_slice_in_dim(x, row, 1, axis=dim), axis, [(0, 1), (1, 0)])
        return got, got
    up = [(i, (i + 1) % size) for i in range(size - 1)]
    down = [(j, i) for i, j in up]
    last = lax.slice_in_dim(x, length - 1, length, axis=dim)
    first = lax.slice_in_dim(x, 0, 1, axis=dim)
    before = lax.ppermute(last, axis, up)
    after = lax.ppermute(first, axis, down)
    return before, after


def padded_band(above, band_rows, below, axis):
    if lax.axis_size(axis) == 2:
        position = lax.axis_index(axis)
        zero = jnp.zeros_like(above)
        above = jnp.where(position == 1, above, zero)
        below = jnp.where(position == 0, below, zero)
    return jnp.concatenate([above, band_rows, below], axis=0)


def conv_taps(x, w_ref):
    rows = x.shape[0] - 2
    width, k = x.shape[1], x.shape[2]
    m = w_ref.shape[3]
    n = rows * width
    lhs = jnp.concatenate([x[a : a + rows].reshape(n, k) for a in range(3)], axis=1)
    weight = jnp.concatenate(
        [jnp.concatenate([w_ref[a, b] for b in range(3)], axis=1) for a in range(3)], axis=0
    )
    acc = jnp.dot(lhs, weight, preferred_element_type=jnp.float32)
    column = lax.broadcasted_iota(jnp.int32, (n, m), 0) % width
    from_left = pltpu.roll(acc[:, :m], 1, 0)
    from_right = pltpu.roll(acc[:, 2 * m :], n - 1, 0)
    total = acc[:, m : 2 * m]
    total = total + jnp.where(column == 0, 0.0, from_left)
    total = total + jnp.where(column == width - 1, 0.0, from_right)
    return total


def input_kernel(
    decay_ref,
    top_ref,
    frame_ref,
    bottom_ref,
    w_ref,
    out_ref,
    cum_ref,
    send_ref,
    state_ref,
    power_ref,
):
    f = pl.program_id(0)
    band, width, m = out_ref.shape[1:]
    cells = band * width

    @pl.when(f == 0)
    def _():
        state_ref[...] = jnp.zeros_like(state_ref)
        power_ref[...] = jnp.ones_like(power_ref)

    x = padded_band(top_ref[f], frame_ref[0], bottom_ref[f], "rows")
    drive = conv_taps(x, w_ref)
    rate = decay_ref[pl.ds(f, 1), :]
    state = rate * state_ref[...] + drive
    power = rate * power_ref[...]
    state_ref[...] = state
    power_ref[...] = power
    out_ref[0] = state.reshape(band, width, m)
    cum_ref[pl.ds(f, 1), :] = power

    @pl.when(f == pl.num_programs(0) - 1)
    def _():
        hi = power.astype(jnp.bfloat16)
        rest = power - hi.astype(jnp.float32)
        mid = rest.astype(jnp.bfloat16)
        low = (rest - mid.astype(jnp.float32)).astype(jnp.bfloat16)
        pad = send_ref.shape[0] - cells - 3
        send_ref[...] = jnp.concatenate(
            [state.astype(jnp.bfloat16), hi, mid, low, jnp.zeros((pad, m), jnp.bfloat16)], axis=0
        )


def output_kernel(
    cum_ref, skip_ref, incoming_ref, top_ref, local_ref, bottom_ref, frame_ref, w_ref, out_ref
):
    f = pl.program_id(0)
    band, width, m = out_ref.shape[1:]
    inner = (local_ref[0] + cum_ref[pl.ds(f, 1), :] * incoming_ref[...]).astype(jnp.bfloat16)
    x = padded_band(top_ref[f], inner, bottom_ref[f], "rows")
    total = conv_taps(x, w_ref)
    frame = frame_ref[0].reshape(band * width, m).astype(jnp.float32)
    total = total + skip_ref[...] * frame
    out_ref[0] = total.astype(jnp.bfloat16).reshape(band, width, m)


def input_stage(frames, conv_in, decay):
    count, band, width, channels = frames.shape
    state_width = conv_in.shape[3]
    top, bottom = halo_rows(frames, "rows", 1)
    halo = pl.BlockSpec(memory_space=pltpu.VMEM)
    payload_rows = band * width + 16
    return pl.pallas_call(
        input_kernel,
        grid=(count,),
        in_specs=[
            pl.BlockSpec((count, state_width), lambda f: (0, 0)),
            halo,
            pl.BlockSpec((1, band, width, channels), lambda f: (f, 0, 0, 0)),
            halo,
            pl.BlockSpec((3, 3, channels, state_width), lambda f: (0, 0, 0, 0)),
        ],
        out_specs=[
            pl.BlockSpec((1, band, width, state_width), lambda f: (f, 0, 0, 0)),
            pl.BlockSpec((count, state_width), lambda f: (0, 0)),
            pl.BlockSpec((payload_rows, state_width), lambda f: (0, 0)),
        ],
        out_shape=[
            jax.ShapeDtypeStruct((count, band, width, state_width), jnp.float32),
            jax.ShapeDtypeStruct((count, state_width), jnp.float32),
            jax.ShapeDtypeStruct((payload_rows, state_width), jnp.bfloat16),
        ],
        scratch_shapes=[
            pltpu.VMEM((band * width, state_width), jnp.float32),
            pltpu.VMEM((1, state_width), jnp.float32),
        ],
        compiler_params=pltpu.CompilerParams(dimension_semantics=("arbitrary",)),
    )(decay, top, frames, bottom, conv_in)


def output_stage(local, cumulative, incoming, frames, conv_out, skip):
    count, band, width, state_width = local.shape
    channels = conv_out.shape[3]
    edges = jnp.concatenate([local[:, :1], local[:, -1:]], axis=1)
    edges = edges + cumulative[:, None, None, :] * jnp.concatenate(
        [incoming[None, :1], incoming[None, -1:]], axis=1
    )
    top, bottom = halo_rows(edges.astype(jnp.bfloat16), "rows", 1)
    halo = pl.BlockSpec(memory_space=pltpu.VMEM)
    return pl.pallas_call(
        output_kernel,
        grid=(count,),
        in_specs=[
            pl.BlockSpec((count, state_width), lambda f: (0, 0)),
            pl.BlockSpec((1, channels), lambda f: (0, 0)),
            pl.BlockSpec((band, width, state_width), lambda f: (0, 0, 0)),
            halo,
            pl.BlockSpec((1, band, width, state_width), lambda f: (f, 0, 0, 0)),
            halo,
            pl.BlockSpec((1, band, width, channels), lambda f: (f, 0, 0, 0)),
            pl.BlockSpec((3, 3, state_width, channels), lambda f: (0, 0, 0, 0)),
        ],
        out_specs=pl.BlockSpec((1, band, width, channels), lambda f: (f, 0, 0, 0)),
        out_shape=jax.ShapeDtypeStruct((count, band, width, channels), jnp.bfloat16),
        compiler_params=pltpu.CompilerParams(dimension_semantics=("arbitrary",)),
    )(cumulative, skip.reshape(1, channels), incoming, top, local, bottom, frames, conv_out)


def split3(p, rows):
    hi = lax.reduce_precision(p, exponent_bits=8, mantissa_bits=7)
    rest = p - hi
    mid = lax.reduce_precision(rest, exponent_bits=8, mantissa_bits=7)
    low = rest - mid
    parts = jnp.stack([hi, mid, low]).astype(jnp.bfloat16)
    return jnp.pad(parts, ((0, rows - 3), (0, 0)))


def incoming_state(power, state, first_payload, axis):
    n = lax.axis_size(axis)
    rows, width, channels = state.shape
    cells = rows * width
    win_p, win_s = power, state
    acc_p, acc_s = None, None
    payload = first_payload
    shift = 1
    while shift < n:
        pairs = [(i, i + shift) for i in range(n - shift)]
        if payload is None:
            payload = jnp.concatenate(
                [win_s.astype(jnp.bfloat16).reshape(cells, channels), split3(win_p, 16)], axis=0
            )
        got = lax.ppermute(payload, axis, pairs)
        payload = None
        got_s = got[:cells].astype(jnp.float32).reshape(rows, width, channels)
        got_p = jnp.sum(got[cells : cells + 3].astype(jnp.float32), axis=0)
        if acc_s is None:
            acc_p, acc_s = got_p, got_s
        else:
            acc_s = acc_p * got_s + acc_s
            acc_p = got_p * acc_p
        if 2 * shift < n:
            win_s = win_p * got_s + win_s
            win_p = got_p * win_p
        shift *= 2
    if acc_s is None:
        return jnp.zeros_like(state)
    return acc_s


def shards(frames, conv_in, decay, conv_out, skip):
    with jax.named_scope("input_conv_and_recurrence"):
        local, cumulative, first_payload = input_stage(frames, conv_in, decay)
    with jax.named_scope("carry_across_blocks"):
        incoming = incoming_state(cumulative[-1], local[-1], first_payload, "tm")
    with jax.named_scope("output_conv"):
        return output_stage(local, cumulative, incoming, frames, conv_out, skip)


def solution(mesh):
    return jax.shard_map(
        shards,
        mesh=mesh,
        in_specs=(P("tm", "rows", None, None), P(), P("tm", None), P(), P()),
        out_specs=P("tm", "rows", None, None),
        check_vma=False,
    )
```

```python
import jax
import jax.numpy as jnp
from jax import lax
from jax.experimental import pallas as pl
from jax.experimental.pallas import tpu as pltpu
from jax.sharding import PartitionSpec as P


def halo_rows(x, axis, dim):
    size, length = (lax.axis_size(axis), x.shape[dim])
    if size == 2:
        row = (1 - lax.axis_index(axis)) * (length - 1)
        got = lax.ppermute(lax.dynamic_slice_in_dim(x, row, 1, axis=dim), axis, [(0, 1), (1, 0)])
        return got, got
    up = [(i, (i + 1) % size) for i in range(size - 1)]
    down = [(j, i) for i, j in up]
    last = lax.slice_in_dim(x, length - 1, length, axis=dim)
    first = lax.slice_in_dim(x, 0, 1, axis=dim)
    before = lax.ppermute(last, axis, up)
    after = lax.ppermute(first, axis, down)
    return before, after


def padded_band(above, band_rows, below, axis):
    if lax.axis_size(axis) == 2:
        position = lax.axis_index(axis)
        zero = jnp.zeros_like(above)
        above = jnp.where(position == 1, above, zero)
        below = jnp.where(position == 0, below, zero)
    return jnp.concatenate([above, band_rows, below], axis=0)


def conv_taps(x, w_ref):
    rows = x.shape[0] - 2
    width, k = x.shape[1], x.shape[2]
    m = w_ref.shape[3]
    n = rows * width
    lhs = jnp.concatenate([x[a : a + rows].reshape(n, k) for a in range(3)], axis=1)
    weight = jnp.concatenate(
        [jnp.concatenate([w_ref[a, b] for b in range(3)], axis=1) for a in range(3)], axis=0
    )
    acc = jnp.dot(lhs, weight, preferred_element_type=jnp.float32)
    column = lax.broadcasted_iota(jnp.int32, (n, m), 0) % width
    from_left = pltpu.roll(acc[:, :m], 1, 0)
    from_right = pltpu.roll(acc[:, 2 * m :], n - 1, 0)
    total = acc[:, m : 2 * m]
    total = total + jnp.where(column == 0, 0.0, from_left)
    total = total + jnp.where(column == width - 1, 0.0, from_right)
    return total


def input_kernel(
    decay_ref,
    top_ref,
    frame_ref,
    bottom_ref,
    w_ref,
    out_ref,
    cum_ref,
    send_ref,
    block_ref,
    state_ref,
    power_ref,
):
    f = pl.program_id(0)
    band, width, m = out_ref.shape[1:]
    cells = band * width

    @pl.when(f == 0)
    def _():
        state_ref[...] = jnp.zeros_like(state_ref)
        power_ref[...] = jnp.ones_like(power_ref)

    x = padded_band(top_ref[f], frame_ref[0], bottom_ref[f], "rows")
    drive = conv_taps(x, w_ref)
    rate = decay_ref[pl.ds(f, 1), :]
    state = rate * state_ref[...] + drive
    power = rate * power_ref[...]
    state_ref[...] = state
    power_ref[...] = power
    out_ref[0] = state.reshape(band, width, m)
    cum_ref[pl.ds(f, 1), :] = power

    @pl.when(f == pl.num_programs(0) - 1)
    def _():
        hi = power.astype(jnp.bfloat16)
        rest = power - hi.astype(jnp.float32)
        mid = rest.astype(jnp.bfloat16)
        low = (rest - mid.astype(jnp.float32)).astype(jnp.bfloat16)
        block_ref[...] = power
        pad = send_ref.shape[0] - cells - 3
        send_ref[...] = jnp.concatenate(
            [state.astype(jnp.bfloat16), hi, mid, low, jnp.zeros((pad, m), jnp.bfloat16)], axis=0
        )


def output_kernel(
    cum_ref, skip_ref, incoming_ref, top_ref, local_ref, bottom_ref, frame_ref, w_ref, out_ref
):
    f = pl.program_id(0)
    band, width, m = out_ref.shape[1:]
    inner = (local_ref[0] + cum_ref[pl.ds(f, 1), :] * incoming_ref[...]).astype(jnp.bfloat16)
    x = padded_band(top_ref[f], inner, bottom_ref[f], "rows")
    total = conv_taps(x, w_ref)
    frame = frame_ref[0].reshape(band * width, m).astype(jnp.float32)
    total = total + skip_ref[...] * frame
    out_ref[0] = total.astype(jnp.bfloat16).reshape(band, width, m)


def input_stage(frames, conv_in, decay):
    count, band, width, channels = frames.shape
    state_width = conv_in.shape[3]
    top, bottom = halo_rows(frames, "rows", 1)
    halo = pl.BlockSpec(memory_space=pltpu.VMEM)
    payload_rows = band * width + 16
    return pl.pallas_call(
        input_kernel,
        grid=(count,),
        in_specs=[
            pl.BlockSpec((count, state_width), lambda f: (0, 0)),
            halo,
            pl.BlockSpec((1, band, width, channels), lambda f: (f, 0, 0, 0)),
            halo,
            pl.BlockSpec((3, 3, channels, state_width), lambda f: (0, 0, 0, 0)),
        ],
        out_specs=[
            pl.BlockSpec((1, band, width, state_width), lambda f: (f, 0, 0, 0)),
            pl.BlockSpec((count, state_width), lambda f: (0, 0)),
            pl.BlockSpec((payload_rows, state_width), lambda f: (0, 0)),
            pl.BlockSpec((1, state_width), lambda f: (0, 0)),
        ],
        out_shape=[
            jax.ShapeDtypeStruct((count, band, width, state_width), jnp.float32),
            jax.ShapeDtypeStruct((count, state_width), jnp.float32),
            jax.ShapeDtypeStruct((payload_rows, state_width), jnp.bfloat16),
            jax.ShapeDtypeStruct((1, state_width), jnp.float32),
        ],
        scratch_shapes=[
            pltpu.VMEM((band * width, state_width), jnp.float32),
            pltpu.VMEM((1, state_width), jnp.float32),
        ],
        compiler_params=pltpu.CompilerParams(dimension_semantics=("arbitrary",)),
    )(decay, top, frames, bottom, conv_in)


def output_stage(local, cumulative, incoming, frames, conv_out, skip):
    count, band, width, state_width = local.shape
    channels = conv_out.shape[3]
    edges = jnp.concatenate([local[:, :1], local[:, -1:]], axis=1)
    edges = edges + cumulative[:, None, None, :] * jnp.concatenate(
        [incoming[None, :1], incoming[None, -1:]], axis=1
    )
    top, bottom = halo_rows(edges.astype(jnp.bfloat16), "rows", 1)
    halo = pl.BlockSpec(memory_space=pltpu.VMEM)
    return pl.pallas_call(
        output_kernel,
        grid=(count,),
        in_specs=[
            pl.BlockSpec((count, state_width), lambda f: (0, 0)),
            pl.BlockSpec((1, channels), lambda f: (0, 0)),
            pl.BlockSpec((band, width, state_width), lambda f: (0, 0, 0)),
            halo,
            pl.BlockSpec((1, band, width, state_width), lambda f: (f, 0, 0, 0)),
            halo,
            pl.BlockSpec((1, band, width, channels), lambda f: (f, 0, 0, 0)),
            pl.BlockSpec((3, 3, state_width, channels), lambda f: (0, 0, 0, 0)),
        ],
        out_specs=pl.BlockSpec((1, band, width, channels), lambda f: (f, 0, 0, 0)),
        out_shape=jax.ShapeDtypeStruct((count, band, width, channels), jnp.bfloat16),
        compiler_params=pltpu.CompilerParams(dimension_semantics=("arbitrary",)),
    )(cumulative, skip.reshape(1, channels), incoming, top, local, bottom, frames, conv_out)


def split3(p, rows):
    hi = lax.reduce_precision(p, exponent_bits=8, mantissa_bits=7)
    rest = p - hi
    mid = lax.reduce_precision(rest, exponent_bits=8, mantissa_bits=7)
    low = rest - mid
    parts = jnp.stack([hi, mid, low]).astype(jnp.bfloat16)
    return jnp.pad(parts, ((0, rows - 3), (0, 0)))


def incoming_state(power, state, first_payload, axis):
    n = lax.axis_size(axis)
    rows, width, channels = state.shape
    cells = rows * width
    win_p, win_s = power, state
    acc_p, acc_s = None, None
    payload = first_payload
    shift = 1
    while shift < n:
        pairs = [(i, i + shift) for i in range(n - shift)]
        if payload is None:
            payload = jnp.concatenate(
                [win_s.astype(jnp.bfloat16).reshape(cells, channels), split3(win_p, 16)], axis=0
            )
        got = lax.ppermute(payload, axis, pairs)
        payload = None
        got_s = got[:cells].astype(jnp.float32).reshape(rows, width, channels)
        got_p = jnp.sum(got[cells : cells + 3].astype(jnp.float32), axis=0)
        if acc_s is None:
            acc_p, acc_s = got_p, got_s
        else:
            acc_s = acc_p * got_s + acc_s
            acc_p = got_p * acc_p
        if 2 * shift < n:
            win_s = win_p * got_s + win_s
            win_p = got_p * win_p
        shift *= 2
    if acc_s is None:
        return jnp.zeros_like(state)
    return acc_s


def shards(frames, conv_in, decay, conv_out, skip):
    with jax.named_scope("input_conv_and_recurrence"):
        local, cumulative, first_payload, block = input_stage(frames, conv_in, decay)
    with jax.named_scope("carry_across_blocks"):
        incoming = incoming_state(block[0], local[-1], first_payload, "tm")
    with jax.named_scope("output_conv"):
        return output_stage(local, cumulative, incoming, frames, conv_out, skip)


def solution(mesh):
    return jax.shard_map(
        shards,
        mesh=mesh,
        in_specs=(P("tm", "rows", None, None), P(), P("tm", None), P(), P()),
        out_specs=P("tm", "rows", None, None),
        check_vma=False,
    )
```

```python
import jax
import jax.numpy as jnp
from jax import lax
from jax.experimental import pallas as pl
from jax.experimental.pallas import tpu as pltpu
from jax.sharding import PartitionSpec as P


def halo_rows(x, axis, dim):
    size, length = (lax.axis_size(axis), x.shape[dim])
    if size == 2:
        row = (1 - lax.axis_index(axis)) * (length - 1)
        got = lax.ppermute(lax.dynamic_slice_in_dim(x, row, 1, axis=dim), axis, [(0, 1), (1, 0)])
        return got, got
    up = [(i, (i + 1) % size) for i in range(size - 1)]
    down = [(j, i) for i, j in up]
    last = lax.slice_in_dim(x, length - 1, length, axis=dim)
    first = lax.slice_in_dim(x, 0, 1, axis=dim)
    before = lax.ppermute(last, axis, up)
    after = lax.ppermute(first, axis, down)
    return before, after


def padded_band(above, band_rows, below, axis):
    if lax.axis_size(axis) == 2:
        position = lax.axis_index(axis)
        zero = jnp.zeros_like(above)
        above = jnp.where(position == 1, above, zero)
        below = jnp.where(position == 0, below, zero)
    return jnp.concatenate([above, band_rows, below], axis=0)


def conv_taps(x, w_ref):
    rows = x.shape[0] - 2
    width, k = x.shape[1], x.shape[2]
    m = w_ref.shape[3]
    n = rows * width
    lhs = jnp.concatenate([x[a : a + rows].reshape(n, k) for a in range(3)], axis=1)
    weight = jnp.concatenate(
        [jnp.concatenate([w_ref[a, b] for b in range(3)], axis=1) for a in range(3)], axis=0
    )
    acc = jnp.dot(lhs, weight, preferred_element_type=jnp.float32)
    column = lax.broadcasted_iota(jnp.int32, (n, m), 0) % width
    from_left = pltpu.roll(acc[:, :m], 1, 0)
    from_right = pltpu.roll(acc[:, 2 * m :], n - 1, 0)
    total = acc[:, m : 2 * m]
    total = total + jnp.where(column == 0, 0.0, from_left)
    total = total + jnp.where(column == width - 1, 0.0, from_right)
    return total


def input_kernel(
    decay_ref,
    top_ref,
    frame_ref,
    bottom_ref,
    w_ref,
    out_ref,
    cum_ref,
    send_ref,
    state_ref,
    power_ref,
):
    f = pl.program_id(0)
    band, width, m = out_ref.shape[1:]
    cells = band * width

    @pl.when(f == 0)
    def _():
        state_ref[...] = jnp.zeros_like(state_ref)
        power_ref[...] = jnp.ones_like(power_ref)

    x = padded_band(top_ref[f], frame_ref[0], bottom_ref[f], "rows")
    drive = conv_taps(x, w_ref)
    rate = decay_ref[pl.ds(f, 1), :]
    state = rate * state_ref[...] + drive
    power = rate * power_ref[...]
    state_ref[...] = state
    power_ref[...] = power
    out_ref[0] = state.reshape(band, width, m)
    cum_ref[pl.ds(f, 1), :] = power

    @pl.when(f == pl.num_programs(0) - 1)
    def _():
        hi = power.astype(jnp.bfloat16)
        rest = power - hi.astype(jnp.float32)
        mid = rest.astype(jnp.bfloat16)
        low = (rest - mid.astype(jnp.float32)).astype(jnp.bfloat16)
        pad = send_ref.shape[0] - cells - 3
        send_ref[...] = jnp.concatenate(
            [state.astype(jnp.bfloat16), hi, mid, low, jnp.zeros((pad, m), jnp.bfloat16)], axis=0
        )


def output_kernel(
    cum_ref, skip_ref, incoming_ref, top_ref, local_ref, bottom_ref, frame_ref, w_ref, out_ref
):
    f = pl.program_id(0)
    band, width, m = out_ref.shape[1:]
    inner = (local_ref[0] + cum_ref[pl.ds(f, 1), :] * incoming_ref[...]).astype(jnp.bfloat16)
    x = padded_band(top_ref[f], inner, bottom_ref[f], "rows")
    total = conv_taps(x, w_ref)
    frame = frame_ref[0].reshape(band * width, m).astype(jnp.float32)
    total = total + skip_ref[...] * frame
    out_ref[0] = total.astype(jnp.bfloat16).reshape(band, width, m)


def input_stage(frames, conv_in, decay):
    count, band, width, channels = frames.shape
    state_width = conv_in.shape[3]
    top, bottom = halo_rows(frames, "rows", 1)
    halo = pl.BlockSpec(memory_space=pltpu.VMEM)
    payload_rows = band * width + 16
    return pl.pallas_call(
        input_kernel,
        grid=(count,),
        in_specs=[
            pl.BlockSpec((count, state_width), lambda f: (0, 0)),
            halo,
            pl.BlockSpec((1, band, width, channels), lambda f: (f, 0, 0, 0)),
            halo,
            pl.BlockSpec((3, 3, channels, state_width), lambda f: (0, 0, 0, 0)),
        ],
        out_specs=[
            pl.BlockSpec((1, band, width, state_width), lambda f: (f, 0, 0, 0)),
            pl.BlockSpec((count, state_width), lambda f: (0, 0)),
            pl.BlockSpec((payload_rows, state_width), lambda f: (0, 0)),
        ],
        out_shape=[
            jax.ShapeDtypeStruct((count, band, width, state_width), jnp.float32),
            jax.ShapeDtypeStruct((count, state_width), jnp.float32),
            jax.ShapeDtypeStruct((payload_rows, state_width), jnp.bfloat16),
        ],
        scratch_shapes=[
            pltpu.VMEM((band * width, state_width), jnp.float32),
            pltpu.VMEM((1, state_width), jnp.float32),
        ],
        compiler_params=pltpu.CompilerParams(dimension_semantics=("arbitrary",)),
    )(decay, top, frames, bottom, conv_in)


def output_stage(local, cumulative, incoming, frames, conv_out, skip):
    count, band, width, state_width = local.shape
    channels = conv_out.shape[3]
    edges = jnp.concatenate([local[:, :1], local[:, -1:]], axis=1)
    edges = edges + cumulative[:, None, None, :] * jnp.concatenate(
        [incoming[None, :1], incoming[None, -1:]], axis=1
    )
    top, bottom = halo_rows(edges.astype(jnp.bfloat16), "rows", 1)
    halo = pl.BlockSpec(memory_space=pltpu.VMEM)
    return pl.pallas_call(
        output_kernel,
        grid=(count,),
        in_specs=[
            pl.BlockSpec((count, state_width), lambda f: (0, 0)),
            pl.BlockSpec((1, channels), lambda f: (0, 0)),
            pl.BlockSpec((band, width, state_width), lambda f: (0, 0, 0)),
            halo,
            pl.BlockSpec((1, band, width, state_width), lambda f: (f, 0, 0, 0)),
            halo,
            pl.BlockSpec((1, band, width, channels), lambda f: (f, 0, 0, 0)),
            pl.BlockSpec((3, 3, state_width, channels), lambda f: (0, 0, 0, 0)),
        ],
        out_specs=pl.BlockSpec((1, band, width, channels), lambda f: (f, 0, 0, 0)),
        out_shape=jax.ShapeDtypeStruct((count, band, width, channels), jnp.bfloat16),
        compiler_params=pltpu.CompilerParams(dimension_semantics=("arbitrary",)),
    )(cumulative, skip.reshape(1, channels), incoming, top, local, bottom, frames, conv_out)


def split3(p, rows):
    hi = lax.reduce_precision(p, exponent_bits=8, mantissa_bits=7)
    rest = p - hi
    mid = lax.reduce_precision(rest, exponent_bits=8, mantissa_bits=7)
    low = rest - mid
    parts = jnp.stack([hi, mid, low]).astype(jnp.bfloat16)
    return jnp.pad(parts, ((0, rows - 3), (0, 0)))


def incoming_state(power, first_payload, axis):
    n = lax.axis_size(axis)
    rows = first_payload.shape[0]
    cells = rows - 16
    win_p = power
    acc_p, acc_s = None, None
    payload = first_payload
    shift = 1
    while shift < n:
        pairs = [(i, i + shift) for i in range(n - shift)]
        got = lax.ppermute(payload, axis, pairs)
        got_s = got[:cells].astype(jnp.float32)
        got_p = jnp.sum(got[cells : cells + 3].astype(jnp.float32), axis=0)
        if acc_s is None:
            acc_p, acc_s = got_p, got_s
        else:
            acc_s = acc_p * got_s + acc_s
            acc_p = got_p * acc_p
        if 2 * shift < n:
            win_s = win_p * got_s + payload[:cells].astype(jnp.float32)
            win_p = got_p * win_p
            payload = jnp.concatenate([win_s.astype(jnp.bfloat16), split3(win_p, 16)], axis=0)
        shift *= 2
    if acc_s is None:
        return jnp.zeros((cells, first_payload.shape[1]), jnp.float32)
    return acc_s


def shards(frames, conv_in, decay, conv_out, skip):
    with jax.named_scope("input_conv_and_recurrence"):
        local, cumulative, first_payload = input_stage(frames, conv_in, decay)
    with jax.named_scope("carry_across_blocks"):
        incoming = incoming_state(cumulative[-1], first_payload, "tm").reshape(local.shape[1:])
    with jax.named_scope("output_conv"):
        return output_stage(local, cumulative, incoming, frames, conv_out, skip)


def solution(mesh):
    return jax.shard_map(
        shards,
        mesh=mesh,
        in_specs=(P("tm", "rows", None, None), P(), P("tm", None), P(), P()),
        out_specs=P("tm", "rows", None, None),
        check_vma=False,
    )
```

```python
import jax
import jax.numpy as jnp
from jax import lax
from jax.experimental import pallas as pl
from jax.experimental.pallas import tpu as pltpu
from jax.sharding import PartitionSpec as P


def halo_rows(x, axis, dim):
    size, length = (lax.axis_size(axis), x.shape[dim])
    if size == 2:
        row = (1 - lax.axis_index(axis)) * (length - 1)
        got = lax.ppermute(lax.dynamic_slice_in_dim(x, row, 1, axis=dim), axis, [(0, 1), (1, 0)])
        return got, got
    up = [(i, (i + 1) % size) for i in range(size - 1)]
    down = [(j, i) for i, j in up]
    last = lax.slice_in_dim(x, length - 1, length, axis=dim)
    first = lax.slice_in_dim(x, 0, 1, axis=dim)
    before = lax.ppermute(last, axis, up)
    after = lax.ppermute(first, axis, down)
    return before, after


def padded_band(above, band_rows, below, axis):
    if lax.axis_size(axis) == 2:
        position = lax.axis_index(axis)
        zero = jnp.zeros_like(above)
        above = jnp.where(position == 1, above, zero)
        below = jnp.where(position == 0, below, zero)
    return jnp.concatenate([above, band_rows, below], axis=0)


def conv_taps(x, w_ref):
    rows = x.shape[0] - 2
    width, k = x.shape[1], x.shape[2]
    m = w_ref.shape[3]
    n = rows * width
    lhs = jnp.concatenate([x[a : a + rows].reshape(n, k) for a in range(3)], axis=1)
    weight = jnp.concatenate(
        [jnp.concatenate([w_ref[a, b] for b in range(3)], axis=1) for a in range(3)], axis=0
    )
    acc = jnp.dot(lhs, weight, preferred_element_type=jnp.float32)
    column = lax.broadcasted_iota(jnp.int32, (n, m), 0) % width
    from_left = pltpu.roll(acc[:, :m], 1, 0)
    from_right = pltpu.roll(acc[:, 2 * m :], n - 1, 0)
    total = acc[:, m : 2 * m]
    total = total + jnp.where(column == 0, 0.0, from_left)
    total = total + jnp.where(column == width - 1, 0.0, from_right)
    return total


def input_kernel(
    decay_ref,
    top_ref,
    frame_ref,
    bottom_ref,
    w_ref,
    out_ref,
    cum_ref,
    send_ref,
    state_ref,
    power_ref,
):
    f = pl.program_id(0)
    band, width, m = out_ref.shape[1:]
    cells = band * width

    @pl.when(f == 0)
    def _():
        state_ref[...] = jnp.zeros_like(state_ref)
        power_ref[...] = jnp.ones_like(power_ref)

    x = padded_band(top_ref[f], frame_ref[0], bottom_ref[f], "rows")
    drive = conv_taps(x, w_ref)
    rate = decay_ref[pl.ds(f, 1), :]
    state = rate * state_ref[...] + drive
    power = rate * power_ref[...]
    state_ref[...] = state
    power_ref[...] = power
    out_ref[0] = state.reshape(band, width, m)
    cum_ref[pl.ds(f, 1), :] = power

    @pl.when(f == pl.num_programs(0) - 1)
    def _():
        hi = power.astype(jnp.bfloat16)
        rest = power - hi.astype(jnp.float32)
        mid = rest.astype(jnp.bfloat16)
        low = (rest - mid.astype(jnp.float32)).astype(jnp.bfloat16)
        pad = send_ref.shape[0] - cells - 3
        send_ref[...] = jnp.concatenate(
            [state.astype(jnp.bfloat16), hi, mid, low, jnp.zeros((pad, m), jnp.bfloat16)], axis=0
        )


def output_kernel(
    cum_ref, skip_ref, incoming_ref, top_ref, local_ref, bottom_ref, frame_ref, w_ref, out_ref
):
    f = pl.program_id(0)
    band, width, m = out_ref.shape[1:]
    inner = (local_ref[0] + cum_ref[pl.ds(f, 1), :] * incoming_ref[...]).astype(jnp.bfloat16)
    x = padded_band(top_ref[f], inner, bottom_ref[f], "rows")
    total = conv_taps(x, w_ref)
    frame = frame_ref[0].reshape(band * width, m).astype(jnp.float32)
    total = total + skip_ref[...] * frame
    out_ref[0] = total.astype(jnp.bfloat16).reshape(band, width, m)


def input_stage(frames, conv_in, decay):
    count, band, width, channels = frames.shape
    state_width = conv_in.shape[3]
    top, bottom = halo_rows(frames, "rows", 1)
    halo = pl.BlockSpec(memory_space=pltpu.VMEM)
    payload_rows = band * width + 16
    return pl.pallas_call(
        input_kernel,
        grid=(count,),
        in_specs=[
            pl.BlockSpec((count, state_width), lambda f: (0, 0)),
            halo,
            pl.BlockSpec((1, band, width, channels), lambda f: (f, 0, 0, 0)),
            halo,
            pl.BlockSpec((3, 3, channels, state_width), lambda f: (0, 0, 0, 0)),
        ],
        out_specs=[
            pl.BlockSpec((1, band, width, state_width), lambda f: (f, 0, 0, 0)),
            pl.BlockSpec((count, state_width), lambda f: (0, 0)),
            pl.BlockSpec((payload_rows, state_width), lambda f: (0, 0)),
        ],
        out_shape=[
            jax.ShapeDtypeStruct((count, band, width, state_width), jnp.float32),
            jax.ShapeDtypeStruct((count, state_width), jnp.float32),
            jax.ShapeDtypeStruct((payload_rows, state_width), jnp.bfloat16),
        ],
        scratch_shapes=[
            pltpu.VMEM((band * width, state_width), jnp.float32),
            pltpu.VMEM((1, state_width), jnp.float32),
        ],
        compiler_params=pltpu.CompilerParams(dimension_semantics=("arbitrary",)),
    )(decay, top, frames, bottom, conv_in)


def output_stage(local, cumulative, incoming, frames, conv_out, skip):
    count, band, width, state_width = local.shape
    channels = conv_out.shape[3]
    edges = jnp.concatenate([local[:, :1], local[:, -1:]], axis=1)
    edges = edges + cumulative[:, None, None, :] * jnp.concatenate(
        [incoming[None, :1], incoming[None, -1:]], axis=1
    )
    top, bottom = halo_rows(edges.astype(jnp.bfloat16), "rows", 1)
    halo = pl.BlockSpec(memory_space=pltpu.VMEM)
    return pl.pallas_call(
        output_kernel,
        grid=(count,),
        in_specs=[
            pl.BlockSpec((count, state_width), lambda f: (0, 0)),
            pl.BlockSpec((1, channels), lambda f: (0, 0)),
            pl.BlockSpec((band, width, state_width), lambda f: (0, 0, 0)),
            halo,
            pl.BlockSpec((1, band, width, state_width), lambda f: (f, 0, 0, 0)),
            halo,
            pl.BlockSpec((1, band, width, channels), lambda f: (f, 0, 0, 0)),
            pl.BlockSpec((3, 3, state_width, channels), lambda f: (0, 0, 0, 0)),
        ],
        out_specs=pl.BlockSpec((1, band, width, channels), lambda f: (f, 0, 0, 0)),
        out_shape=jax.ShapeDtypeStruct((count, band, width, channels), jnp.bfloat16),
        compiler_params=pltpu.CompilerParams(dimension_semantics=("arbitrary",)),
    )(cumulative, skip.reshape(1, channels), incoming, top, local, bottom, frames, conv_out)


def split3(p, rows):
    hi = lax.reduce_precision(p, exponent_bits=8, mantissa_bits=7)
    rest = p - hi
    mid = lax.reduce_precision(rest, exponent_bits=8, mantissa_bits=7)
    low = rest - mid
    parts = jnp.stack([hi, mid, low]).astype(jnp.bfloat16)
    return jnp.pad(parts, ((0, rows - 3), (0, 0)))


def incoming_state(power, state, first_payload, axis):
    n = lax.axis_size(axis)
    me = lax.axis_index(axis)
    rows, width, channels = state.shape
    cells = rows * width
    tot_p, tot_s = power, state.reshape(cells, channels)
    acc_p, acc_s = None, None
    payload = first_payload
    bit = 1
    while bit < n:
        pairs = [(i, i ^ bit) for i in range(n)]
        if payload is None:
            payload = jnp.concatenate([tot_s.astype(jnp.bfloat16), split3(tot_p, 16)], axis=0)
        got = lax.ppermute(payload, axis, pairs)
        payload = None
        got_s = got[:cells].astype(jnp.float32)
        got_p = jnp.sum(got[cells : cells + 3].astype(jnp.float32), axis=0)
        earlier = (me & bit) != 0
        if acc_s is None:
            acc_p = jnp.where(earlier, got_p, jnp.ones_like(got_p))
            acc_s = jnp.where(earlier, got_s, jnp.zeros_like(got_s))
        else:
            acc_s = jnp.where(earlier, acc_p * got_s + acc_s, acc_s)
            acc_p = jnp.where(earlier, got_p * acc_p, acc_p)
        if 2 * bit < n:
            tot_s = jnp.where(earlier, tot_p * got_s + tot_s, got_p * tot_s + got_s)
            tot_p = got_p * tot_p
        bit *= 2
    if acc_s is None:
        return jnp.zeros_like(state)
    return acc_s.reshape(rows, width, channels)


def shards(frames, conv_in, decay, conv_out, skip):
    with jax.named_scope("input_conv_and_recurrence"):
        local, cumulative, first_payload = input_stage(frames, conv_in, decay)
    with jax.named_scope("carry_across_blocks"):
        incoming = incoming_state(cumulative[-1], local[-1], first_payload, "tm")
    with jax.named_scope("output_conv"):
        return output_stage(local, cumulative, incoming, frames, conv_out, skip)


def solution(mesh):
    return jax.shard_map(
        shards,
        mesh=mesh,
        in_specs=(P("tm", "rows", None, None), P(), P("tm", None), P(), P()),
        out_specs=P("tm", "rows", None, None),
        check_vma=False,
    )
```

```python
import jax
import jax.numpy as jnp
from jax import lax
from jax.experimental import pallas as pl
from jax.experimental.pallas import tpu as pltpu
from jax.sharding import PartitionSpec as P


def halo_rows(x, axis, dim):
    size, length = (lax.axis_size(axis), x.shape[dim])
    if size == 2:
        row = (1 - lax.axis_index(axis)) * (length - 1)
        got = lax.ppermute(lax.dynamic_slice_in_dim(x, row, 1, axis=dim), axis, [(0, 1), (1, 0)])
        return got, got
    up = [(i, (i + 1) % size) for i in range(size - 1)]
    down = [(j, i) for i, j in up]
    last = lax.slice_in_dim(x, length - 1, length, axis=dim)
    first = lax.slice_in_dim(x, 0, 1, axis=dim)
    before = lax.ppermute(last, axis, up)
    after = lax.ppermute(first, axis, down)
    return before, after


def padded_band(above, band_rows, below, axis):
    if lax.axis_size(axis) == 2:
        position = lax.axis_index(axis)
        zero = jnp.zeros_like(above)
        above = jnp.where(position == 1, above, zero)
        below = jnp.where(position == 0, below, zero)
    return jnp.concatenate([above, band_rows, below], axis=0)


def conv_taps(x, w_ref):
    rows = x.shape[0] - 2
    width, k = x.shape[1], x.shape[2]
    m = w_ref.shape[3]
    n = rows * width
    lhs = jnp.concatenate([x[a : a + rows].reshape(n, k) for a in range(3)], axis=1)
    weight = jnp.concatenate(
        [jnp.concatenate([w_ref[a, b] for b in range(3)], axis=1) for a in range(3)], axis=0
    )
    acc = jnp.dot(lhs, weight, preferred_element_type=jnp.float32)
    column = lax.broadcasted_iota(jnp.int32, (n, m), 0) % width
    from_left = pltpu.roll(acc[:, :m], 1, 0)
    from_right = pltpu.roll(acc[:, 2 * m :], n - 1, 0)
    total = acc[:, m : 2 * m]
    total = total + jnp.where(column == 0, 0.0, from_left)
    total = total + jnp.where(column == width - 1, 0.0, from_right)
    return total


def input_kernel(
    decay_ref,
    top_ref,
    frame_ref,
    bottom_ref,
    w_ref,
    out_ref,
    cum_ref,
    send_ref,
    state_ref,
    power_ref,
):
    f = pl.program_id(0)
    band, width, m = out_ref.shape[1:]
    cells = band * width

    @pl.when(f == 0)
    def _():
        state_ref[...] = jnp.zeros_like(state_ref)
        power_ref[...] = jnp.ones_like(power_ref)

    x = padded_band(top_ref[f], frame_ref[0], bottom_ref[f], "rows")
    drive = conv_taps(x, w_ref)
    rate = decay_ref[pl.ds(f, 1), :]
    state = rate * state_ref[...] + drive
    power = rate * power_ref[...]
    state_ref[...] = state
    power_ref[...] = power
    out_ref[0] = state.reshape(band, width, m)
    cum_ref[pl.ds(f, 1), :] = power

    @pl.when(f == pl.num_programs(0) - 1)
    def _():
        hi = power.astype(jnp.bfloat16)
        rest = power - hi.astype(jnp.float32)
        mid = rest.astype(jnp.bfloat16)
        low = (rest - mid.astype(jnp.float32)).astype(jnp.bfloat16)
        pad = send_ref.shape[0] - cells - 3
        send_ref[...] = jnp.concatenate(
            [state.astype(jnp.bfloat16), hi, mid, low, jnp.zeros((pad, m), jnp.bfloat16)], axis=0
        )


def output_kernel(
    cum_ref, skip_ref, incoming_ref, top_ref, local_ref, bottom_ref, frame_ref, w_ref, out_ref
):
    f = pl.program_id(0)
    band, width, m = out_ref.shape[1:]
    inner = (local_ref[0] + cum_ref[pl.ds(f, 1), :] * incoming_ref[...]).astype(jnp.bfloat16)
    x = padded_band(top_ref[f], inner, bottom_ref[f], "rows")
    total = conv_taps(x, w_ref)
    frame = frame_ref[0].reshape(band * width, m).astype(jnp.float32)
    total = total + skip_ref[...] * frame
    out_ref[0] = total.astype(jnp.bfloat16).reshape(band, width, m)


def input_stage(frames, conv_in, decay):
    count, band, width, channels = frames.shape
    state_width = conv_in.shape[3]
    top, bottom = halo_rows(frames, "rows", 1)
    halo = pl.BlockSpec(memory_space=pltpu.VMEM)
    payload_rows = band * width + 16
    return pl.pallas_call(
        input_kernel,
        grid=(count,),
        in_specs=[
            pl.BlockSpec((count, state_width), lambda f: (0, 0)),
            halo,
            pl.BlockSpec((1, band, width, channels), lambda f: (f, 0, 0, 0)),
            halo,
            pl.BlockSpec((3, 3, channels, state_width), lambda f: (0, 0, 0, 0)),
        ],
        out_specs=[
            pl.BlockSpec((1, band, width, state_width), lambda f: (f, 0, 0, 0)),
            pl.BlockSpec((count, state_width), lambda f: (0, 0)),
            pl.BlockSpec((payload_rows, state_width), lambda f: (0, 0)),
        ],
        out_shape=[
            jax.ShapeDtypeStruct((count, band, width, state_width), jnp.float32),
            jax.ShapeDtypeStruct((count, state_width), jnp.float32),
            jax.ShapeDtypeStruct((payload_rows, state_width), jnp.bfloat16),
        ],
        scratch_shapes=[
            pltpu.VMEM((band * width, state_width), jnp.float32),
            pltpu.VMEM((1, state_width), jnp.float32),
        ],
        compiler_params=pltpu.CompilerParams(dimension_semantics=("arbitrary",)),
    )(decay, top, frames, bottom, conv_in)


def output_stage(local, cumulative, incoming, frames, conv_out, skip):
    count, band, width, state_width = local.shape
    channels = conv_out.shape[3]
    edges = jnp.concatenate([local[:, :1], local[:, -1:]], axis=1)
    edges = edges + cumulative[:, None, None, :] * jnp.concatenate(
        [incoming[None, :1], incoming[None, -1:]], axis=1
    )
    top, bottom = halo_rows(edges.astype(jnp.bfloat16), "rows", 1)
    halo = pl.BlockSpec(memory_space=pltpu.VMEM)
    return pl.pallas_call(
        output_kernel,
        grid=(count,),
        in_specs=[
            pl.BlockSpec((count, state_width), lambda f: (0, 0)),
            pl.BlockSpec((1, channels), lambda f: (0, 0)),
            pl.BlockSpec((band, width, state_width), lambda f: (0, 0, 0)),
            halo,
            pl.BlockSpec((1, band, width, state_width), lambda f: (f, 0, 0, 0)),
            halo,
            pl.BlockSpec((1, band, width, channels), lambda f: (f, 0, 0, 0)),
            pl.BlockSpec((3, 3, state_width, channels), lambda f: (0, 0, 0, 0)),
        ],
        out_specs=pl.BlockSpec((1, band, width, channels), lambda f: (f, 0, 0, 0)),
        out_shape=jax.ShapeDtypeStruct((count, band, width, channels), jnp.bfloat16),
        compiler_params=pltpu.CompilerParams(dimension_semantics=("arbitrary",)),
    )(cumulative, skip.reshape(1, channels), incoming, top, local, bottom, frames, conv_out)


def split3(p, rows):
    hi = lax.reduce_precision(p, exponent_bits=8, mantissa_bits=7)
    rest = p - hi
    mid = lax.reduce_precision(rest, exponent_bits=8, mantissa_bits=7)
    low = rest - mid
    parts = jnp.stack([hi, mid, low]).astype(jnp.bfloat16)
    return jnp.pad(parts, ((0, rows - 3), (0, 0)))


def incoming_state(power, state, first_payload, axis):
    n = lax.axis_size(axis)
    me = lax.axis_index(axis)
    rows, width, channels = state.shape
    cells = rows * width
    tot_p, tot_s = power, state.reshape(cells, channels)
    acc_p, acc_s = None, None
    payload = first_payload
    bit = 1
    while bit < n:
        earlier = (me & bit) != 0
        if 2 * bit == n and n >= 4 and acc_s is not None:
            quarter, half = n // 4, cells // 2
            offset = ((me // quarter) % 2) * half
            piece = lax.dynamic_slice_in_dim(tot_s.astype(jnp.bfloat16), offset, half, axis=0)
            got_a = lax.ppermute(piece, axis, [(i, i + 2 * quarter) for i in range(2 * quarter)])
            swap = [(i, i + quarter) for i in range(2 * quarter, 3 * quarter)]
            swap += [(j, i) for i, j in swap]
            got_b = lax.ppermute(got_a, axis, swap)
            third = (me // quarter) == 2
            lower_total = jnp.where(
                third,
                jnp.concatenate([got_a, got_b], axis=0),
                jnp.concatenate([got_b, got_a], axis=0),
            ).astype(jnp.float32)
            acc_s = jnp.where(earlier, acc_p * lower_total + acc_s, acc_s)
            break
        pairs = [(i, i ^ bit) for i in range(n)]
        if payload is None:
            payload = jnp.concatenate([tot_s.astype(jnp.bfloat16), split3(tot_p, 16)], axis=0)
        got = lax.ppermute(payload, axis, pairs)
        payload = None
        got_s = got[:cells].astype(jnp.float32)
        got_p = jnp.sum(got[cells : cells + 3].astype(jnp.float32), axis=0)
        if acc_s is None:
            acc_p = jnp.where(earlier, got_p, jnp.ones_like(got_p))
            acc_s = jnp.where(earlier, got_s, jnp.zeros_like(got_s))
        else:
            acc_s = jnp.where(earlier, acc_p * got_s + acc_s, acc_s)
            acc_p = jnp.where(earlier, got_p * acc_p, acc_p)
        if 2 * bit < n:
            tot_s = jnp.where(earlier, tot_p * got_s + tot_s, got_p * tot_s + got_s)
            tot_p = got_p * tot_p
        bit *= 2
    if acc_s is None:
        return jnp.zeros_like(state)
    return acc_s.reshape(rows, width, channels)


def shards(frames, conv_in, decay, conv_out, skip):
    with jax.named_scope("input_conv_and_recurrence"):
        local, cumulative, first_payload = input_stage(frames, conv_in, decay)
    with jax.named_scope("carry_across_blocks"):
        incoming = incoming_state(cumulative[-1], local[-1], first_payload, "tm")
    with jax.named_scope("output_conv"):
        return output_stage(local, cumulative, incoming, frames, conv_out, skip)


def solution(mesh):
    return jax.shard_map(
        shards,
        mesh=mesh,
        in_specs=(P("tm", "rows", None, None), P(), P("tm", None), P(), P()),
        out_specs=P("tm", "rows", None, None),
        check_vma=False,
    )
```

```python
import jax
import jax.numpy as jnp
from jax import lax
from jax.experimental import pallas as pl
from jax.experimental.pallas import tpu as pltpu
from jax.sharding import PartitionSpec as P


def halo_rows(x, axis, dim):
    size, length = (lax.axis_size(axis), x.shape[dim])
    if size == 2:
        row = (1 - lax.axis_index(axis)) * (length - 1)
        got = lax.ppermute(lax.dynamic_slice_in_dim(x, row, 1, axis=dim), axis, [(0, 1), (1, 0)])
        return got, got
    up = [(i, (i + 1) % size) for i in range(size - 1)]
    down = [(j, i) for i, j in up]
    last = lax.slice_in_dim(x, length - 1, length, axis=dim)
    first = lax.slice_in_dim(x, 0, 1, axis=dim)
    before = lax.ppermute(last, axis, up)
    after = lax.ppermute(first, axis, down)
    return before, after


def padded_band(above, band_rows, below, axis):
    if lax.axis_size(axis) == 2:
        position = lax.axis_index(axis)
        zero = jnp.zeros_like(above)
        above = jnp.where(position == 1, above, zero)
        below = jnp.where(position == 0, below, zero)
    return jnp.concatenate([above, band_rows, below], axis=0)


def conv_taps(x, w_ref):
    rows = x.shape[0] - 2
    width, k = x.shape[1], x.shape[2]
    m = w_ref.shape[3]
    n = rows * width
    lhs = jnp.concatenate([x[a : a + rows].reshape(n, k) for a in range(3)], axis=1)
    weight = jnp.concatenate(
        [jnp.concatenate([w_ref[a, b] for b in range(3)], axis=1) for a in range(3)], axis=0
    )
    acc = jnp.dot(lhs, weight, preferred_element_type=jnp.float32)
    column = lax.broadcasted_iota(jnp.int32, (n, m), 0) % width
    from_left = pltpu.roll(acc[:, :m], 1, 0)
    from_right = pltpu.roll(acc[:, 2 * m :], n - 1, 0)
    total = acc[:, m : 2 * m]
    total = total + jnp.where(column == 0, 0.0, from_left)
    total = total + jnp.where(column == width - 1, 0.0, from_right)
    return total


def input_kernel(
    decay_ref,
    top_ref,
    frame_ref,
    bottom_ref,
    w_ref,
    out_ref,
    cum_ref,
    send_ref,
    state_ref,
    power_ref,
):
    f = pl.program_id(0)
    band, width, m = out_ref.shape[1:]
    cells = band * width

    @pl.when(f == 0)
    def _():
        state_ref[...] = jnp.zeros_like(state_ref)
        power_ref[...] = jnp.ones_like(power_ref)

    x = padded_band(top_ref[f], frame_ref[0], bottom_ref[f], "rows")
    drive = conv_taps(x, w_ref)
    rate = decay_ref[pl.ds(f, 1), :]
    state = rate * state_ref[...] + drive
    power = rate * power_ref[...]
    state_ref[...] = state
    power_ref[...] = power
    out_ref[0] = state.reshape(band, width, m)
    cum_ref[pl.ds(f, 1), :] = power

    @pl.when(f == pl.num_programs(0) - 1)
    def _():
        hi = power.astype(jnp.bfloat16)
        rest = power - hi.astype(jnp.float32)
        mid = rest.astype(jnp.bfloat16)
        low = (rest - mid.astype(jnp.float32)).astype(jnp.bfloat16)
        pad = send_ref.shape[0] - cells - 3
        send_ref[...] = jnp.concatenate(
            [state.astype(jnp.bfloat16), hi, mid, low, jnp.zeros((pad, m), jnp.bfloat16)], axis=0
        )


def output_kernel(
    cum_ref, skip_ref, incoming_ref, top_ref, local_ref, bottom_ref, frame_ref, w_ref, out_ref
):
    f = pl.program_id(0)
    band, width, m = out_ref.shape[1:]
    inner = (local_ref[0] + cum_ref[pl.ds(f, 1), :] * incoming_ref[...]).astype(jnp.bfloat16)
    x = padded_band(top_ref[f], inner, bottom_ref[f], "rows")
    total = conv_taps(x, w_ref)
    frame = frame_ref[0].reshape(band * width, m).astype(jnp.float32)
    total = total + skip_ref[...] * frame
    out_ref[0] = total.astype(jnp.bfloat16).reshape(band, width, m)


def input_stage(frames, conv_in, decay):
    count, band, width, channels = frames.shape
    state_width = conv_in.shape[3]
    top, bottom = halo_rows(frames, "rows", 1)
    halo = pl.BlockSpec(memory_space=pltpu.VMEM)
    payload_rows = band * width + 16
    return pl.pallas_call(
        input_kernel,
        grid=(count,),
        in_specs=[
            pl.BlockSpec((count, state_width), lambda f: (0, 0)),
            halo,
            pl.BlockSpec((1, band, width, channels), lambda f: (f, 0, 0, 0)),
            halo,
            pl.BlockSpec((3, 3, channels, state_width), lambda f: (0, 0, 0, 0)),
        ],
        out_specs=[
            pl.BlockSpec((1, band, width, state_width), lambda f: (f, 0, 0, 0)),
            pl.BlockSpec((count, state_width), lambda f: (0, 0)),
            pl.BlockSpec((payload_rows, state_width), lambda f: (0, 0)),
        ],
        out_shape=[
            jax.ShapeDtypeStruct((count, band, width, state_width), jnp.float32),
            jax.ShapeDtypeStruct((count, state_width), jnp.float32),
            jax.ShapeDtypeStruct((payload_rows, state_width), jnp.bfloat16),
        ],
        scratch_shapes=[
            pltpu.VMEM((band * width, state_width), jnp.float32),
            pltpu.VMEM((1, state_width), jnp.float32),
        ],
        compiler_params=pltpu.CompilerParams(dimension_semantics=("arbitrary",)),
    )(decay, top, frames, bottom, conv_in)


def output_stage(local, cumulative, incoming, frames, conv_out, skip):
    count, band, width, state_width = local.shape
    channels = conv_out.shape[3]
    edges = jnp.concatenate([local[:, :1], local[:, -1:]], axis=1)
    edges = edges + cumulative[:, None, None, :] * jnp.concatenate(
        [incoming[None, :1], incoming[None, -1:]], axis=1
    )
    top, bottom = halo_rows(edges.astype(jnp.bfloat16), "rows", 1)
    halo = pl.BlockSpec(memory_space=pltpu.VMEM)
    return pl.pallas_call(
        output_kernel,
        grid=(count,),
        in_specs=[
            pl.BlockSpec((count, state_width), lambda f: (0, 0)),
            pl.BlockSpec((1, channels), lambda f: (0, 0)),
            pl.BlockSpec((band, width, state_width), lambda f: (0, 0, 0)),
            halo,
            pl.BlockSpec((1, band, width, state_width), lambda f: (f, 0, 0, 0)),
            halo,
            pl.BlockSpec((1, band, width, channels), lambda f: (f, 0, 0, 0)),
            pl.BlockSpec((3, 3, state_width, channels), lambda f: (0, 0, 0, 0)),
        ],
        out_specs=pl.BlockSpec((1, band, width, channels), lambda f: (f, 0, 0, 0)),
        out_shape=jax.ShapeDtypeStruct((count, band, width, channels), jnp.bfloat16),
        compiler_params=pltpu.CompilerParams(dimension_semantics=("arbitrary",)),
    )(cumulative, skip.reshape(1, channels), incoming, top, local, bottom, frames, conv_out)


def split3(p, rows):
    hi = lax.reduce_precision(p, exponent_bits=8, mantissa_bits=7)
    rest = p - hi
    mid = lax.reduce_precision(rest, exponent_bits=8, mantissa_bits=7)
    low = rest - mid
    parts = jnp.stack([hi, mid, low]).astype(jnp.bfloat16)
    return jnp.pad(parts, ((0, rows - 3), (0, 0)))


def incoming_state(power, state, first_payload, axis):
    n = lax.axis_size(axis)
    me = lax.axis_index(axis)
    rows, width, channels = state.shape
    cells = rows * width
    tot_p, tot_s = power, state.reshape(cells, channels)
    acc_p, acc_s = None, None
    payload = first_payload
    bit = 1
    while bit < n:
        pairs = [(i, i ^ bit) for i in range(n)]
        if 2 * bit == n:
            pairs = [(i, i + bit) for i in range(bit)]
        if payload is None:
            payload = jnp.concatenate([tot_s.astype(jnp.bfloat16), split3(tot_p, 16)], axis=0)
        got = lax.ppermute(payload, axis, pairs)
        payload = None
        got_s = got[:cells].astype(jnp.float32)
        got_p = jnp.sum(got[cells : cells + 3].astype(jnp.float32), axis=0)
        earlier = (me & bit) != 0
        if acc_s is None:
            acc_p = jnp.where(earlier, got_p, jnp.ones_like(got_p))
            acc_s = jnp.where(earlier, got_s, jnp.zeros_like(got_s))
        else:
            acc_s = jnp.where(earlier, acc_p * got_s + acc_s, acc_s)
            acc_p = jnp.where(earlier, got_p * acc_p, acc_p)
        if 2 * bit < n:
            tot_s = jnp.where(earlier, tot_p * got_s + tot_s, got_p * tot_s + got_s)
            tot_p = got_p * tot_p
        bit *= 2
    if acc_s is None:
        return jnp.zeros_like(state)
    return acc_s.reshape(rows, width, channels)


def shards(frames, conv_in, decay, conv_out, skip):
    with jax.named_scope("input_conv_and_recurrence"):
        local, cumulative, first_payload = input_stage(frames, conv_in, decay)
    with jax.named_scope("carry_across_blocks"):
        incoming = incoming_state(cumulative[-1], local[-1], first_payload, "tm")
    with jax.named_scope("output_conv"):
        return output_stage(local, cumulative, incoming, frames, conv_out, skip)


def solution(mesh):
    return jax.shard_map(
        shards,
        mesh=mesh,
        in_specs=(P("tm", "rows", None, None), P(), P("tm", None), P(), P()),
        out_specs=P("tm", "rows", None, None),
        check_vma=False,
    )
```

```python
import jax
import jax.numpy as jnp
from jax import lax
from jax.experimental import pallas as pl
from jax.experimental.pallas import tpu as pltpu
from jax.sharding import PartitionSpec as P


def halo_rows(x, axis, dim):
    size, length = (lax.axis_size(axis), x.shape[dim])
    if size == 2:
        row = (1 - lax.axis_index(axis)) * (length - 1)
        got = lax.ppermute(lax.dynamic_slice_in_dim(x, row, 1, axis=dim), axis, [(0, 1), (1, 0)])
        return got, got
    up = [(i, (i + 1) % size) for i in range(size - 1)]
    down = [(j, i) for i, j in up]
    last = lax.slice_in_dim(x, length - 1, length, axis=dim)
    first = lax.slice_in_dim(x, 0, 1, axis=dim)
    before = lax.ppermute(last, axis, up)
    after = lax.ppermute(first, axis, down)
    return before, after


def padded_band(above, band_rows, below, axis):
    if lax.axis_size(axis) == 2:
        position = lax.axis_index(axis)
        zero = jnp.zeros_like(above)
        above = jnp.where(position == 1, above, zero)
        below = jnp.where(position == 0, below, zero)
    return jnp.concatenate([above, band_rows, below], axis=0)


def conv_taps(x, w_ref):
    rows = x.shape[0] - 2
    width, k = x.shape[1], x.shape[2]
    m = w_ref.shape[3]
    n = rows * width
    lhs = jnp.concatenate([x[a : a + rows].reshape(n, k) for a in range(3)], axis=1)
    weight = jnp.concatenate(
        [jnp.concatenate([w_ref[a, b] for b in range(3)], axis=1) for a in range(3)], axis=0
    )
    acc = jnp.dot(lhs, weight, preferred_element_type=jnp.float32)
    column = lax.broadcasted_iota(jnp.int32, (n, m), 0) % width
    from_left = pltpu.roll(acc[:, :m], 1, 0)
    from_right = pltpu.roll(acc[:, 2 * m :], n - 1, 0)
    total = acc[:, m : 2 * m]
    total = total + jnp.where(column == 0, 0.0, from_left)
    total = total + jnp.where(column == width - 1, 0.0, from_right)
    return total


def input_kernel(
    decay_ref,
    top_ref,
    frame_ref,
    bottom_ref,
    w_ref,
    out_ref,
    cum_ref,
    send_ref,
    state_ref,
    power_ref,
):
    f = pl.program_id(0)
    band, width, m = out_ref.shape[1:]
    cells = band * width

    @pl.when(f == 0)
    def _():
        state_ref[...] = jnp.zeros_like(state_ref)
        power_ref[...] = jnp.ones_like(power_ref)

    x = padded_band(top_ref[f], frame_ref[0], bottom_ref[f], "rows")
    drive = conv_taps(x, w_ref)
    rate = decay_ref[pl.ds(f, 1), :]
    state = rate * state_ref[...] + drive
    power = rate * power_ref[...]
    state_ref[...] = state
    power_ref[...] = power
    out_ref[0] = state.reshape(band, width, m)
    cum_ref[pl.ds(f, 1), :] = power

    @pl.when(f == pl.num_programs(0) - 1)
    def _():
        hi = power.astype(jnp.bfloat16)
        rest = power - hi.astype(jnp.float32)
        mid = rest.astype(jnp.bfloat16)
        low = (rest - mid.astype(jnp.float32)).astype(jnp.bfloat16)
        pad = send_ref.shape[0] - cells - 3
        send_ref[...] = jnp.concatenate(
            [state.astype(jnp.bfloat16), hi, mid, low, jnp.zeros((pad, m), jnp.bfloat16)], axis=0
        )


def output_kernel(
    cum_ref, skip_ref, incoming_ref, top_ref, local_ref, bottom_ref, frame_ref, w_ref, out_ref
):
    f = pl.program_id(0)
    band, width, m = out_ref.shape[1:]
    inner = (local_ref[0] + cum_ref[pl.ds(f, 1), :] * incoming_ref[...]).astype(jnp.bfloat16)
    x = padded_band(top_ref[f], inner, bottom_ref[f], "rows")
    total = conv_taps(x, w_ref)
    frame = frame_ref[0].reshape(band * width, m).astype(jnp.float32)
    total = total + skip_ref[...] * frame
    out_ref[0] = total.astype(jnp.bfloat16).reshape(band, width, m)


def input_stage(frames, conv_in, decay):
    count, band, width, channels = frames.shape
    state_width = conv_in.shape[3]
    top, bottom = halo_rows(frames, "rows", 1)
    halo = pl.BlockSpec(memory_space=pltpu.VMEM)
    payload_rows = band * width + 16
    return pl.pallas_call(
        input_kernel,
        grid=(count,),
        in_specs=[
            pl.BlockSpec((count, state_width), lambda f: (0, 0)),
            halo,
            pl.BlockSpec((1, band, width, channels), lambda f: (f, 0, 0, 0)),
            halo,
            pl.BlockSpec((3, 3, channels, state_width), lambda f: (0, 0, 0, 0)),
        ],
        out_specs=[
            pl.BlockSpec((1, band, width, state_width), lambda f: (f, 0, 0, 0)),
            pl.BlockSpec((count, state_width), lambda f: (0, 0)),
            pl.BlockSpec((payload_rows, state_width), lambda f: (0, 0)),
        ],
        out_shape=[
            jax.ShapeDtypeStruct((count, band, width, state_width), jnp.float32),
            jax.ShapeDtypeStruct((count, state_width), jnp.float32),
            jax.ShapeDtypeStruct((payload_rows, state_width), jnp.bfloat16),
        ],
        scratch_shapes=[
            pltpu.VMEM((band * width, state_width), jnp.float32),
            pltpu.VMEM((1, state_width), jnp.float32),
        ],
        compiler_params=pltpu.CompilerParams(dimension_semantics=("arbitrary",)),
    )(decay, top, frames, bottom, conv_in)


def output_stage(local, cumulative, incoming, frames, conv_out, skip):
    count, band, width, state_width = local.shape
    channels = conv_out.shape[3]
    edges = jnp.concatenate([local[:, :1], local[:, -1:]], axis=1)
    edges = edges + cumulative[:, None, None, :] * jnp.concatenate(
        [incoming[None, :1], incoming[None, -1:]], axis=1
    )
    top, bottom = halo_rows(edges.astype(jnp.bfloat16), "rows", 1)
    halo = pl.BlockSpec(memory_space=pltpu.VMEM)
    return pl.pallas_call(
        output_kernel,
        grid=(count,),
        in_specs=[
            pl.BlockSpec((count, state_width), lambda f: (0, 0)),
            pl.BlockSpec((1, channels), lambda f: (0, 0)),
            pl.BlockSpec((band, width, state_width), lambda f: (0, 0, 0)),
            halo,
            pl.BlockSpec((1, band, width, state_width), lambda f: (f, 0, 0, 0)),
            halo,
            pl.BlockSpec((1, band, width, channels), lambda f: (f, 0, 0, 0)),
            pl.BlockSpec((3, 3, state_width, channels), lambda f: (0, 0, 0, 0)),
        ],
        out_specs=pl.BlockSpec((1, band, width, channels), lambda f: (f, 0, 0, 0)),
        out_shape=jax.ShapeDtypeStruct((count, band, width, channels), jnp.bfloat16),
        compiler_params=pltpu.CompilerParams(dimension_semantics=("arbitrary",)),
    )(cumulative, skip.reshape(1, channels), incoming, top, local, bottom, frames, conv_out)


def split3(p, rows):
    hi = lax.reduce_precision(p, exponent_bits=8, mantissa_bits=7)
    rest = p - hi
    mid = lax.reduce_precision(rest, exponent_bits=8, mantissa_bits=7)
    low = rest - mid
    parts = jnp.stack([hi, mid, low]).astype(jnp.bfloat16)
    return jnp.pad(parts, ((0, rows - 3), (0, 0)))


def incoming_state(power, state, first_payload, axis):
    n = lax.axis_size(axis)
    me = lax.axis_index(axis)
    rows, width, channels = state.shape
    cells = rows * width
    tot_p, tot_s = power, state.reshape(cells, channels)
    acc_p, acc_s = None, None
    payload = first_payload
    bit = 1
    while bit < n:
        pairs = [(i, i ^ bit) for i in range(n)]
        if payload is None:
            payload = jnp.concatenate([tot_s.astype(jnp.bfloat16), split3(tot_p, 16)], axis=0)
        got = lax.ppermute(payload, axis, pairs)
        payload = None
        got_s = got[:cells].astype(jnp.float32)
        got_p = jnp.sum(got[cells : cells + 3].astype(jnp.float32), axis=0)
        earlier = (me & bit) != 0
        if acc_s is None:
            acc_p = jnp.where(earlier, got_p, jnp.ones_like(got_p))
            acc_s = jnp.where(earlier, got_s, jnp.zeros_like(got_s))
        else:
            acc_s = jnp.where(earlier, acc_p * got_s + acc_s, acc_s)
            acc_p = jnp.where(earlier, got_p * acc_p, acc_p)
        if 2 * bit < n:
            tot_s = jnp.where(earlier, tot_p * got_s + tot_s, got_p * tot_s + got_s)
            tot_p = got_p * tot_p
        bit *= 2
    if acc_s is None:
        return jnp.zeros_like(state)
    return acc_s.reshape(rows, width, channels)


def shards(frames, conv_in, decay, conv_out, skip):
    with jax.named_scope("block_decay_product"):
        block_power = decay[0]
        for frame_index in range(1, decay.shape[0]):
            block_power = block_power * decay[frame_index]
    with jax.named_scope("input_conv_and_recurrence"):
        local, cumulative, first_payload = input_stage(frames, conv_in, decay)
    with jax.named_scope("carry_across_blocks"):
        incoming = incoming_state(block_power, local[-1], first_payload, "tm")
    with jax.named_scope("output_conv"):
        return output_stage(local, cumulative, incoming, frames, conv_out, skip)


def solution(mesh):
    return jax.shard_map(
        shards,
        mesh=mesh,
        in_specs=(P("tm", "rows", None, None), P(), P("tm", None), P(), P()),
        out_specs=P("tm", "rows", None, None),
        check_vma=False,
    )
```

```python
import jax
import jax.numpy as jnp
from jax import lax
from jax.experimental import pallas as pl
from jax.experimental.pallas import tpu as pltpu
from jax.sharding import PartitionSpec as P

PER_STEP = 2


def halo_rows(x, axis, dim):
    size, length = (lax.axis_size(axis), x.shape[dim])
    if size == 2:
        row = (1 - lax.axis_index(axis)) * (length - 1)
        got = lax.ppermute(lax.dynamic_slice_in_dim(x, row, 1, axis=dim), axis, [(0, 1), (1, 0)])
        return got, got
    up = [(i, (i + 1) % size) for i in range(size - 1)]
    down = [(j, i) for i, j in up]
    last = lax.slice_in_dim(x, length - 1, length, axis=dim)
    first = lax.slice_in_dim(x, 0, 1, axis=dim)
    before = lax.ppermute(last, axis, up)
    after = lax.ppermute(first, axis, down)
    return before, after


def padded_band(above, band_rows, below, axis):
    if lax.axis_size(axis) == 2:
        position = lax.axis_index(axis)
        zero = jnp.zeros_like(above)
        above = jnp.where(position == 1, above, zero)
        below = jnp.where(position == 0, below, zero)
    return jnp.concatenate([above, band_rows, below], axis=0)


def conv_taps(x, w_ref):
    rows = x.shape[0] - 2
    width, k = x.shape[1], x.shape[2]
    m = w_ref.shape[3]
    n = rows * width
    lhs = jnp.concatenate([x[a : a + rows].reshape(n, k) for a in range(3)], axis=1)
    weight = jnp.concatenate(
        [jnp.concatenate([w_ref[a, b] for b in range(3)], axis=1) for a in range(3)], axis=0
    )
    acc = jnp.dot(lhs, weight, preferred_element_type=jnp.float32)
    column = lax.broadcasted_iota(jnp.int32, (n, m), 0) % width
    from_left = pltpu.roll(acc[:, :m], 1, 0)
    from_right = pltpu.roll(acc[:, 2 * m :], n - 1, 0)
    total = acc[:, m : 2 * m]
    total = total + jnp.where(column == 0, 0.0, from_left)
    total = total + jnp.where(column == width - 1, 0.0, from_right)
    return total


def input_kernel(
    decay_ref,
    top_ref,
    frame_ref,
    bottom_ref,
    w_ref,
    out_ref,
    cum_ref,
    send_ref,
    state_ref,
    power_ref,
):
    f = pl.program_id(0)
    band, width, m = out_ref.shape[1:]
    cells = band * width

    @pl.when(f == 0)
    def _():
        state_ref[...] = jnp.zeros_like(state_ref)
        power_ref[...] = jnp.ones_like(power_ref)

    per = frame_ref.shape[0]
    state = state_ref[...]
    power = power_ref[...]
    for j in range(per):
        g = f * per + j
        x = padded_band(top_ref[g], frame_ref[j], bottom_ref[g], "rows")
        drive = conv_taps(x, w_ref)
        rate = decay_ref[pl.ds(g, 1), :]
        state = rate * state + drive
        power = rate * power
        out_ref[j] = state.reshape(band, width, m)
        cum_ref[pl.ds(g, 1), :] = power
    state_ref[...] = state
    power_ref[...] = power

    @pl.when(f == pl.num_programs(0) - 1)
    def _():
        hi = power.astype(jnp.bfloat16)
        rest = power - hi.astype(jnp.float32)
        mid = rest.astype(jnp.bfloat16)
        low = (rest - mid.astype(jnp.float32)).astype(jnp.bfloat16)
        pad = send_ref.shape[0] - cells - 3
        send_ref[...] = jnp.concatenate(
            [state.astype(jnp.bfloat16), hi, mid, low, jnp.zeros((pad, m), jnp.bfloat16)], axis=0
        )


def output_kernel(
    cum_ref, skip_ref, incoming_ref, top_ref, local_ref, bottom_ref, frame_ref, w_ref, out_ref
):
    f = pl.program_id(0)
    band, width, m = out_ref.shape[1:]
    per = frame_ref.shape[0]
    for j in range(per):
        g = f * per + j
        inner = (local_ref[j] + cum_ref[pl.ds(g, 1), :] * incoming_ref[...]).astype(jnp.bfloat16)
        x = padded_band(top_ref[g], inner, bottom_ref[g], "rows")
        total = conv_taps(x, w_ref)
        frame = frame_ref[j].reshape(band * width, m).astype(jnp.float32)
        total = total + skip_ref[...] * frame
        out_ref[j] = total.astype(jnp.bfloat16).reshape(band, width, m)


def input_stage(frames, conv_in, decay):
    count, band, width, channels = frames.shape
    state_width = conv_in.shape[3]
    top, bottom = halo_rows(frames, "rows", 1)
    halo = pl.BlockSpec(memory_space=pltpu.VMEM)
    payload_rows = band * width + 16
    return pl.pallas_call(
        input_kernel,
        grid=(count // PER_STEP,),
        in_specs=[
            pl.BlockSpec((count, state_width), lambda f: (0, 0)),
            halo,
            pl.BlockSpec((PER_STEP, band, width, channels), lambda f: (f, 0, 0, 0)),
            halo,
            pl.BlockSpec((3, 3, channels, state_width), lambda f: (0, 0, 0, 0)),
        ],
        out_specs=[
            pl.BlockSpec((PER_STEP, band, width, state_width), lambda f: (f, 0, 0, 0)),
            pl.BlockSpec((count, state_width), lambda f: (0, 0)),
            pl.BlockSpec((payload_rows, state_width), lambda f: (0, 0)),
        ],
        out_shape=[
            jax.ShapeDtypeStruct((count, band, width, state_width), jnp.float32),
            jax.ShapeDtypeStruct((count, state_width), jnp.float32),
            jax.ShapeDtypeStruct((payload_rows, state_width), jnp.bfloat16),
        ],
        scratch_shapes=[
            pltpu.VMEM((band * width, state_width), jnp.float32),
            pltpu.VMEM((1, state_width), jnp.float32),
        ],
        compiler_params=pltpu.CompilerParams(dimension_semantics=("arbitrary",)),
    )(decay, top, frames, bottom, conv_in)


def output_stage(local, cumulative, incoming, frames, conv_out, skip):
    count, band, width, state_width = local.shape
    channels = conv_out.shape[3]
    edges = jnp.concatenate([local[:, :1], local[:, -1:]], axis=1)
    edges = edges + cumulative[:, None, None, :] * jnp.concatenate(
        [incoming[None, :1], incoming[None, -1:]], axis=1
    )
    top, bottom = halo_rows(edges.astype(jnp.bfloat16), "rows", 1)
    halo = pl.BlockSpec(memory_space=pltpu.VMEM)
    return pl.pallas_call(
        output_kernel,
        grid=(count // PER_STEP,),
        in_specs=[
            pl.BlockSpec((count, state_width), lambda f: (0, 0)),
            pl.BlockSpec((1, channels), lambda f: (0, 0)),
            pl.BlockSpec((band, width, state_width), lambda f: (0, 0, 0)),
            halo,
            pl.BlockSpec((PER_STEP, band, width, state_width), lambda f: (f, 0, 0, 0)),
            halo,
            pl.BlockSpec((PER_STEP, band, width, channels), lambda f: (f, 0, 0, 0)),
            pl.BlockSpec((3, 3, state_width, channels), lambda f: (0, 0, 0, 0)),
        ],
        out_specs=pl.BlockSpec((PER_STEP, band, width, channels), lambda f: (f, 0, 0, 0)),
        out_shape=jax.ShapeDtypeStruct((count, band, width, channels), jnp.bfloat16),
        compiler_params=pltpu.CompilerParams(dimension_semantics=("arbitrary",)),
    )(cumulative, skip.reshape(1, channels), incoming, top, local, bottom, frames, conv_out)


def split3(p, rows):
    hi = lax.reduce_precision(p, exponent_bits=8, mantissa_bits=7)
    rest = p - hi
    mid = lax.reduce_precision(rest, exponent_bits=8, mantissa_bits=7)
    low = rest - mid
    parts = jnp.stack([hi, mid, low]).astype(jnp.bfloat16)
    return jnp.pad(parts, ((0, rows - 3), (0, 0)))


def incoming_state(power, state, first_payload, axis):
    n = lax.axis_size(axis)
    me = lax.axis_index(axis)
    rows, width, channels = state.shape
    cells = rows * width
    tot_p, tot_s = power, state.reshape(cells, channels)
    acc_p, acc_s = None, None
    payload = first_payload
    bit = 1
    while bit < n:
        pairs = [(i, i ^ bit) for i in range(n)]
        if payload is None:
            payload = jnp.concatenate([tot_s.astype(jnp.bfloat16), split3(tot_p, 16)], axis=0)
        got = lax.ppermute(payload, axis, pairs)
        payload = None
        got_s = got[:cells].astype(jnp.float32)
        got_p = jnp.sum(got[cells : cells + 3].astype(jnp.float32), axis=0)
        earlier = (me & bit) != 0
        if acc_s is None:
            acc_p = jnp.where(earlier, got_p, jnp.ones_like(got_p))
            acc_s = jnp.where(earlier, got_s, jnp.zeros_like(got_s))
        else:
            acc_s = jnp.where(earlier, acc_p * got_s + acc_s, acc_s)
            acc_p = jnp.where(earlier, got_p * acc_p, acc_p)
        if 2 * bit < n:
            tot_s = jnp.where(earlier, tot_p * got_s + tot_s, got_p * tot_s + got_s)
            tot_p = got_p * tot_p
        bit *= 2
    if acc_s is None:
        return jnp.zeros_like(state)
    return acc_s.reshape(rows, width, channels)


def shards(frames, conv_in, decay, conv_out, skip):
    with jax.named_scope("block_decay_product"):
        block_power = decay[0]
        for frame_index in range(1, decay.shape[0]):
            block_power = block_power * decay[frame_index]
    with jax.named_scope("input_conv_and_recurrence"):
        local, cumulative, first_payload = input_stage(frames, conv_in, decay)
    with jax.named_scope("carry_across_blocks"):
        incoming = incoming_state(block_power, local[-1], first_payload, "tm")
    with jax.named_scope("output_conv"):
        return output_stage(local, cumulative, incoming, frames, conv_out, skip)


def solution(mesh):
    return jax.shard_map(
        shards,
        mesh=mesh,
        in_specs=(P("tm", "rows", None, None), P(), P("tm", None), P(), P()),
        out_specs=P("tm", "rows", None, None),
        check_vma=False,
    )
```

```python
import jax
import jax.numpy as jnp
from jax import lax
from jax.experimental import pallas as pl
from jax.experimental.pallas import tpu as pltpu
from jax.sharding import PartitionSpec as P

PER_STEP = 2


def halo_rows(x, axis, dim):
    size, length = (lax.axis_size(axis), x.shape[dim])
    if size == 2:
        row = (1 - lax.axis_index(axis)) * (length - 1)
        got = lax.ppermute(lax.dynamic_slice_in_dim(x, row, 1, axis=dim), axis, [(0, 1), (1, 0)])
        return got, got
    up = [(i, (i + 1) % size) for i in range(size - 1)]
    down = [(j, i) for i, j in up]
    last = lax.slice_in_dim(x, length - 1, length, axis=dim)
    first = lax.slice_in_dim(x, 0, 1, axis=dim)
    before = lax.ppermute(last, axis, up)
    after = lax.ppermute(first, axis, down)
    return before, after


def padded_band(above, band_rows, below, axis):
    if lax.axis_size(axis) == 2:
        position = lax.axis_index(axis)
        zero = jnp.zeros_like(above)
        above = jnp.where(position == 1, above, zero)
        below = jnp.where(position == 0, below, zero)
    return jnp.concatenate([above, band_rows, below], axis=0)


def conv_taps(x, w_ref):
    rows = x.shape[0] - 2
    width, k = x.shape[1], x.shape[2]
    m = w_ref.shape[3]
    n = rows * width
    lhs = jnp.concatenate([x[a : a + rows].reshape(n, k) for a in range(3)], axis=1)
    weight = jnp.concatenate(
        [jnp.concatenate([w_ref[a, b] for b in range(3)], axis=1) for a in range(3)], axis=0
    )
    acc = jnp.dot(lhs, weight, preferred_element_type=jnp.float32)
    column = lax.broadcasted_iota(jnp.int32, (n, m), 0) % width
    from_left = pltpu.roll(acc[:, :m], 1, 0)
    from_right = pltpu.roll(acc[:, 2 * m :], n - 1, 0)
    total = acc[:, m : 2 * m]
    total = total + jnp.where(column == 0, 0.0, from_left)
    total = total + jnp.where(column == width - 1, 0.0, from_right)
    return total


def input_kernel(
    decay_ref,
    top_ref,
    frame_ref,
    bottom_ref,
    w_ref,
    out_ref,
    cum_ref,
    send_ref,
    state_ref,
    power_ref,
):
    f = pl.program_id(0)
    band, width, m = out_ref.shape[1:]
    cells = band * width

    @pl.when(f == 0)
    def _():
        state_ref[...] = jnp.zeros_like(state_ref)
        power_ref[...] = jnp.ones_like(power_ref)

    per = frame_ref.shape[0]
    state = state_ref[...]
    power = power_ref[...]
    for j in range(per):
        g = f * per + j
        x = padded_band(top_ref[g], frame_ref[j], bottom_ref[g], "rows")
        drive = conv_taps(x, w_ref)
        rate = decay_ref[pl.ds(g, 1), :]
        state = rate * state + drive
        power = rate * power
        out_ref[j] = state.reshape(band, width, m)
        cum_ref[pl.ds(g, 1), :] = power
    state_ref[...] = state
    power_ref[...] = power

    @pl.when(f == pl.num_programs(0) - 1)
    def _():
        hi = power.astype(jnp.bfloat16)
        rest = power - hi.astype(jnp.float32)
        mid = rest.astype(jnp.bfloat16)
        low = (rest - mid.astype(jnp.float32)).astype(jnp.bfloat16)
        pad = send_ref.shape[0] - cells - 3
        send_ref[...] = jnp.concatenate(
            [state.astype(jnp.bfloat16), hi, mid, low, jnp.zeros((pad, m), jnp.bfloat16)], axis=0
        )


def output_kernel(cum_ref, skip_ref, incoming_ref, local_ref, frame_ref, w_ref, out_ref, rim_ref):
    f = pl.program_id(0)
    band, width, m = out_ref.shape[1:]
    per = frame_ref.shape[0]
    for j in range(per):
        g = f * per + j
        inner = (local_ref[j] + cum_ref[pl.ds(g, 1), :] * incoming_ref[...]).astype(jnp.bfloat16)
        zero = jnp.zeros((1, width, inner.shape[2]), jnp.bfloat16)
        total = conv_taps(jnp.concatenate([zero, inner, zero], axis=0), w_ref)
        frame = frame_ref[j].reshape(band * width, m).astype(jnp.float32)
        total = total + skip_ref[...] * frame
        out_ref[j] = total.astype(jnp.bfloat16).reshape(band, width, m)
        rim_ref[j, 0] = total[:width]
        rim_ref[j, 1] = total[(band - 1) * width :]


def halo_effect(rows_2d, w_ref, a, width):
    m = w_ref.shape[3]
    taps = jnp.concatenate([w_ref[a, b] for b in range(3)], axis=1)
    acc = jnp.dot(rows_2d, taps, preferred_element_type=jnp.float32)
    n = acc.shape[0]
    column = lax.broadcasted_iota(jnp.int32, (n, m), 0) % width
    from_left = pltpu.roll(acc[:, :m], 1, 0)
    from_right = pltpu.roll(acc[:, 2 * m :], n - 1, 0)
    total = acc[:, m : 2 * m]
    total = total + jnp.where(column == 0, 0.0, from_left)
    return total + jnp.where(column == width - 1, 0.0, from_right)


def output_edge_kernel(rim_ref, top_ref, bottom_ref, w_ref, body_ref, out_ref, upper_buf, lower_buf, sems):
    del body_ref
    count, _, width, m = rim_ref.shape
    band = out_ref.shape[1]
    k = top_ref.shape[3]
    above = top_ref[...].reshape(count * width, k)
    below = bottom_ref[...].reshape(count * width, k)
    up = halo_effect(above, w_ref, 0, width)
    down = halo_effect(below, w_ref, 2, width)
    if lax.axis_size("rows") == 2:
        position = lax.axis_index("rows")
        up = jnp.where(position == 1, up, 0.0)
        down = jnp.where(position == 0, down, 0.0)
    rim = rim_ref[...]
    upper_buf[...] = (rim[:, 0].reshape(count * width, m) + up).astype(jnp.bfloat16).reshape(
        count, 1, width, m
    )
    lower_buf[...] = (rim[:, 1].reshape(count * width, m) + down).astype(jnp.bfloat16).reshape(
        count, 1, width, m
    )
    copies = [
        pltpu.make_async_copy(upper_buf, out_ref.at[:, pl.ds(0, 1)], sems.at[0]),
        pltpu.make_async_copy(lower_buf, out_ref.at[:, pl.ds(band - 1, 1)], sems.at[1]),
    ]
    for copy in copies:
        copy.start()
    for copy in copies:
        copy.wait()


def input_stage(frames, conv_in, decay):
    count, band, width, channels = frames.shape
    state_width = conv_in.shape[3]
    top, bottom = halo_rows(frames, "rows", 1)
    halo = pl.BlockSpec(memory_space=pltpu.VMEM)
    payload_rows = band * width + 16
    return pl.pallas_call(
        input_kernel,
        grid=(count // PER_STEP,),
        in_specs=[
            pl.BlockSpec((count, state_width), lambda f: (0, 0)),
            halo,
            pl.BlockSpec((PER_STEP, band, width, channels), lambda f: (f, 0, 0, 0)),
            halo,
            pl.BlockSpec((3, 3, channels, state_width), lambda f: (0, 0, 0, 0)),
        ],
        out_specs=[
            pl.BlockSpec((PER_STEP, band, width, state_width), lambda f: (f, 0, 0, 0)),
            pl.BlockSpec((count, state_width), lambda f: (0, 0)),
            pl.BlockSpec((payload_rows, state_width), lambda f: (0, 0)),
        ],
        out_shape=[
            jax.ShapeDtypeStruct((count, band, width, state_width), jnp.float32),
            jax.ShapeDtypeStruct((count, state_width), jnp.float32),
            jax.ShapeDtypeStruct((payload_rows, state_width), jnp.bfloat16),
        ],
        scratch_shapes=[
            pltpu.VMEM((band * width, state_width), jnp.float32),
            pltpu.VMEM((1, state_width), jnp.float32),
        ],
        compiler_params=pltpu.CompilerParams(dimension_semantics=("arbitrary",)),
    )(decay, top, frames, bottom, conv_in)


def output_stage(local, cumulative, incoming, frames, conv_out, skip):
    count, band, width, state_width = local.shape
    channels = conv_out.shape[3]
    edges = jnp.concatenate([local[:, :1], local[:, -1:]], axis=1)
    edges = edges + cumulative[:, None, None, :] * jnp.concatenate(
        [incoming[None, :1], incoming[None, -1:]], axis=1
    )
    top, bottom = halo_rows(edges.astype(jnp.bfloat16), "rows", 1)
    body, rim = pl.pallas_call(
        output_kernel,
        grid=(count // PER_STEP,),
        in_specs=[
            pl.BlockSpec((count, state_width), lambda f: (0, 0)),
            pl.BlockSpec((1, channels), lambda f: (0, 0)),
            pl.BlockSpec((band, width, state_width), lambda f: (0, 0, 0)),
            pl.BlockSpec((PER_STEP, band, width, state_width), lambda f: (f, 0, 0, 0)),
            pl.BlockSpec((PER_STEP, band, width, channels), lambda f: (f, 0, 0, 0)),
            pl.BlockSpec((3, 3, state_width, channels), lambda f: (0, 0, 0, 0)),
        ],
        out_specs=[
            pl.BlockSpec((PER_STEP, band, width, channels), lambda f: (f, 0, 0, 0)),
            pl.BlockSpec((PER_STEP, 2, width, channels), lambda f: (f, 0, 0, 0)),
        ],
        out_shape=[
            jax.ShapeDtypeStruct((count, band, width, channels), jnp.bfloat16),
            jax.ShapeDtypeStruct((count, 2, width, channels), jnp.float32),
        ],
        compiler_params=pltpu.CompilerParams(dimension_semantics=("arbitrary",)),
    )(cumulative, skip.reshape(1, channels), incoming, local, frames, conv_out)
    vmem = pl.BlockSpec(memory_space=pltpu.VMEM)
    return pl.pallas_call(
        output_edge_kernel,
        in_specs=[vmem, vmem, vmem, vmem, pl.BlockSpec(memory_space=pl.ANY)],
        out_specs=pl.BlockSpec(memory_space=pl.ANY),
        out_shape=jax.ShapeDtypeStruct((count, band, width, channels), jnp.bfloat16),
        scratch_shapes=[
            pltpu.VMEM((count, 1, width, channels), jnp.bfloat16),
            pltpu.VMEM((count, 1, width, channels), jnp.bfloat16),
            pltpu.SemaphoreType.DMA((2,)),
        ],
        input_output_aliases={4: 0},
    )(rim, top, bottom, conv_out, body)


def split3(p, rows):
    hi = lax.reduce_precision(p, exponent_bits=8, mantissa_bits=7)
    rest = p - hi
    mid = lax.reduce_precision(rest, exponent_bits=8, mantissa_bits=7)
    low = rest - mid
    parts = jnp.stack([hi, mid, low]).astype(jnp.bfloat16)
    return jnp.pad(parts, ((0, rows - 3), (0, 0)))


def incoming_state(power, state, first_payload, axis):
    n = lax.axis_size(axis)
    me = lax.axis_index(axis)
    rows, width, channels = state.shape
    cells = rows * width
    tot_p, tot_s = power, state.reshape(cells, channels)
    acc_p, acc_s = None, None
    payload = first_payload
    bit = 1
    while bit < n:
        pairs = [(i, i ^ bit) for i in range(n)]
        if payload is None:
            payload = jnp.concatenate([tot_s.astype(jnp.bfloat16), split3(tot_p, 16)], axis=0)
        got = lax.ppermute(payload, axis, pairs)
        payload = None
        got_s = got[:cells].astype(jnp.float32)
        got_p = jnp.sum(got[cells : cells + 3].astype(jnp.float32), axis=0)
        earlier = (me & bit) != 0
        if acc_s is None:
            acc_p = jnp.where(earlier, got_p, jnp.ones_like(got_p))
            acc_s = jnp.where(earlier, got_s, jnp.zeros_like(got_s))
        else:
            acc_s = jnp.where(earlier, acc_p * got_s + acc_s, acc_s)
            acc_p = jnp.where(earlier, got_p * acc_p, acc_p)
        if 2 * bit < n:
            tot_s = jnp.where(earlier, tot_p * got_s + tot_s, got_p * tot_s + got_s)
            tot_p = got_p * tot_p
        bit *= 2
    if acc_s is None:
        return jnp.zeros_like(state)
    return acc_s.reshape(rows, width, channels)


def shards(frames, conv_in, decay, conv_out, skip):
    with jax.named_scope("block_decay_product"):
        block_power = decay[0]
        for frame_index in range(1, decay.shape[0]):
            block_power = block_power * decay[frame_index]
    with jax.named_scope("input_conv_and_recurrence"):
        local, cumulative, first_payload = input_stage(frames, conv_in, decay)
    with jax.named_scope("carry_across_blocks"):
        incoming = incoming_state(block_power, local[-1], first_payload, "tm")
    with jax.named_scope("output_conv"):
        return output_stage(local, cumulative, incoming, frames, conv_out, skip)


def solution(mesh):
    return jax.shard_map(
        shards,
        mesh=mesh,
        in_specs=(P("tm", "rows", None, None), P(), P("tm", None), P(), P()),
        out_specs=P("tm", "rows", None, None),
        check_vma=False,
    )
```

```python
import functools

import jax
import jax.numpy as jnp
from jax import lax
from jax.experimental import pallas as pl
from jax.experimental.pallas import tpu as pltpu
from jax.sharding import PartitionSpec as P

PER_STEP = 2


def halo_rows(x, axis, dim):
    size, length = (lax.axis_size(axis), x.shape[dim])
    if size == 2:
        row = (1 - lax.axis_index(axis)) * (length - 1)
        got = lax.ppermute(lax.dynamic_slice_in_dim(x, row, 1, axis=dim), axis, [(0, 1), (1, 0)])
        return got, got
    up = [(i, (i + 1) % size) for i in range(size - 1)]
    down = [(j, i) for i, j in up]
    last = lax.slice_in_dim(x, length - 1, length, axis=dim)
    first = lax.slice_in_dim(x, 0, 1, axis=dim)
    before = lax.ppermute(last, axis, up)
    after = lax.ppermute(first, axis, down)
    return before, after


def padded_band(above, band_rows, below, axis):
    if lax.axis_size(axis) == 2:
        position = lax.axis_index(axis)
        zero = jnp.zeros_like(above)
        above = jnp.where(position == 1, above, zero)
        below = jnp.where(position == 0, below, zero)
    return jnp.concatenate([above, band_rows, below], axis=0)


def conv_taps(x, w_ref):
    rows = x.shape[0] - 2
    width, k = x.shape[1], x.shape[2]
    m = w_ref.shape[3]
    n = rows * width
    lhs = jnp.concatenate([x[a : a + rows].reshape(n, k) for a in range(3)], axis=1)
    weight = jnp.concatenate(
        [jnp.concatenate([w_ref[a, b] for b in range(3)], axis=1) for a in range(3)], axis=0
    )
    acc = jnp.dot(lhs, weight, preferred_element_type=jnp.float32)
    column = lax.broadcasted_iota(jnp.int32, (n, m), 0) % width
    from_left = pltpu.roll(acc[:, :m], 1, 0)
    from_right = pltpu.roll(acc[:, 2 * m :], n - 1, 0)
    total = acc[:, m : 2 * m]
    total = total + jnp.where(column == 0, 0.0, from_left)
    total = total + jnp.where(column == width - 1, 0.0, from_right)
    return total


def input_kernel(
    decay_ref,
    top_ref,
    frame_ref,
    bottom_ref,
    w_ref,
    out_ref,
    cum_ref,
    send_ref,
    state_ref,
    power_ref,
):
    f = pl.program_id(0)
    band, width, m = out_ref.shape[1:]
    cells = band * width

    @pl.when(f == 0)
    def _():
        state_ref[...] = jnp.zeros_like(state_ref)
        power_ref[...] = jnp.ones_like(power_ref)

    per = frame_ref.shape[0]
    state = state_ref[...]
    power = power_ref[...]
    for j in range(per):
        g = f * per + j
        x = padded_band(top_ref[g], frame_ref[j], bottom_ref[g], "rows")
        drive = conv_taps(x, w_ref)
        rate = decay_ref[pl.ds(g, 1), :]
        state = rate * state + drive
        power = rate * power
        out_ref[j] = state.reshape(band, width, m)
        cum_ref[pl.ds(g, 1), :] = power
    state_ref[...] = state
    power_ref[...] = power

    @pl.when(f == pl.num_programs(0) - 1)
    def _():
        hi = power.astype(jnp.bfloat16)
        rest = power - hi.astype(jnp.float32)
        mid = rest.astype(jnp.bfloat16)
        low = (rest - mid.astype(jnp.float32)).astype(jnp.bfloat16)
        pad = send_ref.shape[0] - cells - 3
        send_ref[...] = jnp.concatenate(
            [state.astype(jnp.bfloat16), hi, mid, low, jnp.zeros((pad, m), jnp.bfloat16)], axis=0
        )


def output_kernel(
    last_bit,
    cum_ref,
    skip_ref,
    scale_ref,
    got_ref,
    base_ref,
    top_ref,
    local_ref,
    bottom_ref,
    frame_ref,
    w_ref,
    out_ref,
    incoming_ref,
):
    f = pl.program_id(0)

    @pl.when(f == 0)
    def _():
        earlier = (lax.axis_index("tm") & last_bit) != 0
        base = base_ref[...]
        update = scale_ref[...] * got_ref[...].astype(jnp.float32) + base
        incoming_ref[...] = jnp.where(earlier, update, base)

    band, width, m = out_ref.shape[1:]
    per = frame_ref.shape[0]
    for j in range(per):
        g = f * per + j
        inner = (local_ref[j] + cum_ref[pl.ds(g, 1), :] * incoming_ref[...]).astype(jnp.bfloat16)
        x = padded_band(top_ref[g], inner, bottom_ref[g], "rows")
        total = conv_taps(x, w_ref)
        frame = frame_ref[j].reshape(band * width, m).astype(jnp.float32)
        total = total + skip_ref[...] * frame
        out_ref[j] = total.astype(jnp.bfloat16).reshape(band, width, m)


def input_stage(frames, conv_in, decay):
    count, band, width, channels = frames.shape
    state_width = conv_in.shape[3]
    top, bottom = halo_rows(frames, "rows", 1)
    halo = pl.BlockSpec(memory_space=pltpu.VMEM)
    payload_rows = band * width + 16
    return pl.pallas_call(
        input_kernel,
        grid=(count // PER_STEP,),
        in_specs=[
            pl.BlockSpec((count, state_width), lambda f: (0, 0)),
            halo,
            pl.BlockSpec((PER_STEP, band, width, channels), lambda f: (f, 0, 0, 0)),
            halo,
            pl.BlockSpec((3, 3, channels, state_width), lambda f: (0, 0, 0, 0)),
        ],
        out_specs=[
            pl.BlockSpec((PER_STEP, band, width, state_width), lambda f: (f, 0, 0, 0)),
            pl.BlockSpec((count, state_width), lambda f: (0, 0)),
            pl.BlockSpec((payload_rows, state_width), lambda f: (0, 0)),
        ],
        out_shape=[
            jax.ShapeDtypeStruct((count, band, width, state_width), jnp.float32),
            jax.ShapeDtypeStruct((count, state_width), jnp.float32),
            jax.ShapeDtypeStruct((payload_rows, state_width), jnp.bfloat16),
        ],
        scratch_shapes=[
            pltpu.VMEM((band * width, state_width), jnp.float32),
            pltpu.VMEM((1, state_width), jnp.float32),
        ],
        compiler_params=pltpu.CompilerParams(dimension_semantics=("arbitrary",)),
    )(decay, top, frames, bottom, conv_in)


def output_stage(local, cumulative, pieces, frames, conv_out, skip):
    count, band, width, state_width = local.shape
    channels = conv_out.shape[3]
    scale, got_rows, base, last_bit = pieces
    earlier = (lax.axis_index("tm") & last_bit) != 0

    def rows_of(x):
        return jnp.concatenate([x[:1], x[-1:]], axis=0)

    base_rows = rows_of(base)
    incoming_rows = jnp.where(
        earlier, scale * rows_of(got_rows).astype(jnp.float32) + base_rows, base_rows
    )
    edges = jnp.concatenate([local[:, :1], local[:, -1:]], axis=1)
    edges = edges + cumulative[:, None, None, :] * incoming_rows[None]
    top, bottom = halo_rows(edges.astype(jnp.bfloat16), "rows", 1)
    halo = pl.BlockSpec(memory_space=pltpu.VMEM)
    whole_state = pl.BlockSpec((band, width, state_width), lambda f: (0, 0, 0))
    return pl.pallas_call(
        functools.partial(output_kernel, last_bit),
        grid=(count // PER_STEP,),
        in_specs=[
            pl.BlockSpec((count, state_width), lambda f: (0, 0)),
            pl.BlockSpec((1, channels), lambda f: (0, 0)),
            pl.BlockSpec((1, state_width), lambda f: (0, 0)),
            whole_state,
            whole_state,
            halo,
            pl.BlockSpec((PER_STEP, band, width, state_width), lambda f: (f, 0, 0, 0)),
            halo,
            pl.BlockSpec((PER_STEP, band, width, channels), lambda f: (f, 0, 0, 0)),
            pl.BlockSpec((3, 3, state_width, channels), lambda f: (0, 0, 0, 0)),
        ],
        out_specs=pl.BlockSpec((PER_STEP, band, width, channels), lambda f: (f, 0, 0, 0)),
        out_shape=jax.ShapeDtypeStruct((count, band, width, channels), jnp.bfloat16),
        scratch_shapes=[pltpu.VMEM((band, width, state_width), jnp.float32)],
        compiler_params=pltpu.CompilerParams(dimension_semantics=("arbitrary",)),
    )(cumulative, skip.reshape(1, channels), scale, got_rows, base, top, local, bottom, frames, conv_out)


def split3(p, rows):
    hi = lax.reduce_precision(p, exponent_bits=8, mantissa_bits=7)
    rest = p - hi
    mid = lax.reduce_precision(rest, exponent_bits=8, mantissa_bits=7)
    low = rest - mid
    parts = jnp.stack([hi, mid, low]).astype(jnp.bfloat16)
    return jnp.pad(parts, ((0, rows - 3), (0, 0)))


def incoming_state(power, state, first_payload, axis):
    n = lax.axis_size(axis)
    me = lax.axis_index(axis)
    rows, width, channels = state.shape
    cells = rows * width
    tot_p, tot_s = power, state.reshape(cells, channels)
    acc_p = jnp.ones_like(power)
    acc_s = jnp.zeros((cells, channels), jnp.float32)
    payload = first_payload
    last = (acc_p, jnp.zeros((cells, channels), jnp.bfloat16), acc_s, 0)
    bit = 1
    while bit < n:
        pairs = [(i, i ^ bit) for i in range(n)]
        if payload is None:
            payload = jnp.concatenate([tot_s.astype(jnp.bfloat16), split3(tot_p, 16)], axis=0)
        got = lax.ppermute(payload, axis, pairs)
        payload = None
        if 2 * bit >= n:
            last = (acc_p, got[:cells], acc_s, bit)
            break
        got_s = got[:cells].astype(jnp.float32)
        got_p = jnp.sum(got[cells : cells + 3].astype(jnp.float32), axis=0)
        earlier = (me & bit) != 0
        acc_s = jnp.where(earlier, acc_p * got_s + acc_s, acc_s)
        acc_p = jnp.where(earlier, got_p * acc_p, acc_p)
        if 2 * bit < n:
            tot_s = jnp.where(earlier, tot_p * got_s + tot_s, got_p * tot_s + got_s)
            tot_p = got_p * tot_p
        bit *= 2
    scale, got_rows, base, last_bit = last
    shape = (rows, width, channels)
    return scale.reshape(1, channels), got_rows.reshape(shape), base.reshape(shape), last_bit


def shards(frames, conv_in, decay, conv_out, skip):
    with jax.named_scope("block_decay_product"):
        block_power = decay[0]
        for frame_index in range(1, decay.shape[0]):
            block_power = block_power * decay[frame_index]
    with jax.named_scope("input_conv_and_recurrence"):
        local, cumulative, first_payload = input_stage(frames, conv_in, decay)
    with jax.named_scope("carry_across_blocks"):
        pieces = incoming_state(block_power, local[-1], first_payload, "tm")
    with jax.named_scope("output_conv"):
        return output_stage(local, cumulative, pieces, frames, conv_out, skip)


def solution(mesh):
    return jax.shard_map(
        shards,
        mesh=mesh,
        in_specs=(P("tm", "rows", None, None), P(), P("tm", None), P(), P()),
        out_specs=P("tm", "rows", None, None),
        check_vma=False,
    )
```

```python
import jax
import jax.numpy as jnp
from jax import lax
from jax.experimental import pallas as pl
from jax.experimental.pallas import tpu as pltpu
from jax.sharding import PartitionSpec as P

IN_STEP = 4
PER_STEP = 2


def halo_rows(x, axis, dim):
    size, length = (lax.axis_size(axis), x.shape[dim])
    if size == 2:
        row = (1 - lax.axis_index(axis)) * (length - 1)
        got = lax.ppermute(lax.dynamic_slice_in_dim(x, row, 1, axis=dim), axis, [(0, 1), (1, 0)])
        return got, got
    up = [(i, (i + 1) % size) for i in range(size - 1)]
    down = [(j, i) for i, j in up]
    last = lax.slice_in_dim(x, length - 1, length, axis=dim)
    first = lax.slice_in_dim(x, 0, 1, axis=dim)
    before = lax.ppermute(last, axis, up)
    after = lax.ppermute(first, axis, down)
    return before, after


def padded_band(above, band_rows, below, axis):
    if lax.axis_size(axis) == 2:
        position = lax.axis_index(axis)
        zero = jnp.zeros_like(above)
        above = jnp.where(position == 1, above, zero)
        below = jnp.where(position == 0, below, zero)
    return jnp.concatenate([above, band_rows, below], axis=0)


def conv_taps(x, w_ref):
    rows = x.shape[0] - 2
    width, k = x.shape[1], x.shape[2]
    m = w_ref.shape[3]
    n = rows * width
    lhs = jnp.concatenate([x[a : a + rows].reshape(n, k) for a in range(3)], axis=1)
    weight = jnp.concatenate(
        [jnp.concatenate([w_ref[a, b] for b in range(3)], axis=1) for a in range(3)], axis=0
    )
    acc = jnp.dot(lhs, weight, preferred_element_type=jnp.float32)
    column = lax.broadcasted_iota(jnp.int32, (n, m), 0) % width
    from_left = pltpu.roll(acc[:, :m], 1, 0)
    from_right = pltpu.roll(acc[:, 2 * m :], n - 1, 0)
    total = acc[:, m : 2 * m]
    total = total + jnp.where(column == 0, 0.0, from_left)
    total = total + jnp.where(column == width - 1, 0.0, from_right)
    return total


def input_kernel(
    decay_ref,
    top_ref,
    frame_ref,
    bottom_ref,
    w_ref,
    out_ref,
    cum_ref,
    send_ref,
    state_ref,
    power_ref,
):
    f = pl.program_id(0)
    band, width, m = out_ref.shape[1:]
    cells = band * width

    @pl.when(f == 0)
    def _():
        state_ref[...] = jnp.zeros_like(state_ref)
        power_ref[...] = jnp.ones_like(power_ref)

    per = frame_ref.shape[0]
    state = state_ref[...]
    power = power_ref[...]
    for j in range(per):
        g = f * per + j
        x = padded_band(top_ref[g], frame_ref[j], bottom_ref[g], "rows")
        drive = conv_taps(x, w_ref)
        rate = decay_ref[pl.ds(g, 1), :]
        state = rate * state + drive
        power = rate * power
        out_ref[j] = state.reshape(band, width, m)
        cum_ref[pl.ds(g, 1), :] = power
    state_ref[...] = state
    power_ref[...] = power

    @pl.when(f == pl.num_programs(0) - 1)
    def _():
        hi = power.astype(jnp.bfloat16)
        rest = power - hi.astype(jnp.float32)
        mid = rest.astype(jnp.bfloat16)
        low = (rest - mid.astype(jnp.float32)).astype(jnp.bfloat16)
        pad = send_ref.shape[0] - cells - 3
        send_ref[...] = jnp.concatenate(
            [state.astype(jnp.bfloat16), hi, mid, low, jnp.zeros((pad, m), jnp.bfloat16)], axis=0
        )


def output_kernel(
    cum_ref, skip_ref, incoming_ref, top_ref, local_ref, bottom_ref, frame_ref, w_ref, out_ref
):
    f = pl.program_id(0)
    band, width, m = out_ref.shape[1:]
    per = frame_ref.shape[0]
    for j in range(per):
        g = f * per + j
        inner = (local_ref[j] + cum_ref[pl.ds(g, 1), :] * incoming_ref[...]).astype(jnp.bfloat16)
        x = padded_band(top_ref[g], inner, bottom_ref[g], "rows")
        total = conv_taps(x, w_ref)
        frame = frame_ref[j].reshape(band * width, m).astype(jnp.float32)
        total = total + skip_ref[...] * frame
        out_ref[j] = total.astype(jnp.bfloat16).reshape(band, width, m)


def input_stage(frames, conv_in, decay):
    count, band, width, channels = frames.shape
    state_width = conv_in.shape[3]
    top, bottom = halo_rows(frames, "rows", 1)
    halo = pl.BlockSpec(memory_space=pltpu.VMEM)
    payload_rows = band * width + 16
    return pl.pallas_call(
        input_kernel,
        grid=(count // IN_STEP,),
        in_specs=[
            pl.BlockSpec((count, state_width), lambda f: (0, 0)),
            halo,
            pl.BlockSpec((IN_STEP, band, width, channels), lambda f: (f, 0, 0, 0)),
            halo,
            pl.BlockSpec((3, 3, channels, state_width), lambda f: (0, 0, 0, 0)),
        ],
        out_specs=[
            pl.BlockSpec((IN_STEP, band, width, state_width), lambda f: (f, 0, 0, 0)),
            pl.BlockSpec((count, state_width), lambda f: (0, 0)),
            pl.BlockSpec((payload_rows, state_width), lambda f: (0, 0)),
        ],
        out_shape=[
            jax.ShapeDtypeStruct((count, band, width, state_width), jnp.float32),
            jax.ShapeDtypeStruct((count, state_width), jnp.float32),
            jax.ShapeDtypeStruct((payload_rows, state_width), jnp.bfloat16),
        ],
        scratch_shapes=[
            pltpu.VMEM((band * width, state_width), jnp.float32),
            pltpu.VMEM((1, state_width), jnp.float32),
        ],
        compiler_params=pltpu.CompilerParams(dimension_semantics=("arbitrary",)),
    )(decay, top, frames, bottom, conv_in)


def output_stage(local, cumulative, incoming, frames, conv_out, skip):
    count, band, width, state_width = local.shape
    channels = conv_out.shape[3]
    edges = jnp.concatenate([local[:, :1], local[:, -1:]], axis=1)
    edges = edges + cumulative[:, None, None, :] * jnp.concatenate(
        [incoming[None, :1], incoming[None, -1:]], axis=1
    )
    top, bottom = halo_rows(edges.astype(jnp.bfloat16), "rows", 1)
    halo = pl.BlockSpec(memory_space=pltpu.VMEM)
    return pl.pallas_call(
        output_kernel,
        grid=(count // PER_STEP,),
        in_specs=[
            pl.BlockSpec((count, state_width), lambda f: (0, 0)),
            pl.BlockSpec((1, channels), lambda f: (0, 0)),
            pl.BlockSpec((band, width, state_width), lambda f: (0, 0, 0)),
            halo,
            pl.BlockSpec((PER_STEP, band, width, state_width), lambda f: (f, 0, 0, 0)),
            halo,
            pl.BlockSpec((PER_STEP, band, width, channels), lambda f: (f, 0, 0, 0)),
            pl.BlockSpec((3, 3, state_width, channels), lambda f: (0, 0, 0, 0)),
        ],
        out_specs=pl.BlockSpec((PER_STEP, band, width, channels), lambda f: (f, 0, 0, 0)),
        out_shape=jax.ShapeDtypeStruct((count, band, width, channels), jnp.bfloat16),
        compiler_params=pltpu.CompilerParams(dimension_semantics=("arbitrary",)),
    )(cumulative, skip.reshape(1, channels), incoming, top, local, bottom, frames, conv_out)


def split3(p, rows):
    hi = lax.reduce_precision(p, exponent_bits=8, mantissa_bits=7)
    rest = p - hi
    mid = lax.reduce_precision(rest, exponent_bits=8, mantissa_bits=7)
    low = rest - mid
    parts = jnp.stack([hi, mid, low]).astype(jnp.bfloat16)
    return jnp.pad(parts, ((0, rows - 3), (0, 0)))


def incoming_state(power, state, first_payload, axis):
    n = lax.axis_size(axis)
    me = lax.axis_index(axis)
    rows, width, channels = state.shape
    cells = rows * width
    tot_p, tot_s = power, state.reshape(cells, channels)
    acc_p, acc_s = None, None
    payload = first_payload
    bit = 1
    while bit < n:
        pairs = [(i, i ^ bit) for i in range(n)]
        if payload is None:
            payload = jnp.concatenate([tot_s.astype(jnp.bfloat16), split3(tot_p, 16)], axis=0)
        got = lax.ppermute(payload, axis, pairs)
        payload = None
        got_s = got[:cells].astype(jnp.float32)
        got_p = jnp.sum(got[cells : cells + 3].astype(jnp.float32), axis=0)
        earlier = (me & bit) != 0
        if acc_s is None:
            acc_p = jnp.where(earlier, got_p, jnp.ones_like(got_p))
            acc_s = jnp.where(earlier, got_s, jnp.zeros_like(got_s))
        else:
            acc_s = jnp.where(earlier, acc_p * got_s + acc_s, acc_s)
            acc_p = jnp.where(earlier, got_p * acc_p, acc_p)
        if 2 * bit < n:
            tot_s = jnp.where(earlier, tot_p * got_s + tot_s, got_p * tot_s + got_s)
            tot_p = got_p * tot_p
        bit *= 2
    if acc_s is None:
        return jnp.zeros_like(state)
    return acc_s.reshape(rows, width, channels)


def shards(frames, conv_in, decay, conv_out, skip):
    with jax.named_scope("block_decay_product"):
        block_power = decay[0]
        for frame_index in range(1, decay.shape[0]):
            block_power = block_power * decay[frame_index]
    with jax.named_scope("input_conv_and_recurrence"):
        local, cumulative, first_payload = input_stage(frames, conv_in, decay)
    with jax.named_scope("carry_across_blocks"):
        incoming = incoming_state(block_power, local[-1], first_payload, "tm")
    with jax.named_scope("output_conv"):
        return output_stage(local, cumulative, incoming, frames, conv_out, skip)


def solution(mesh):
    return jax.shard_map(
        shards,
        mesh=mesh,
        in_specs=(P("tm", "rows", None, None), P(), P("tm", None), P(), P()),
        out_specs=P("tm", "rows", None, None),
        check_vma=False,
    )
```
